128 devices in a mesh: dp: 32 (over x, z, core), tensor: 4 (over y).
Axes of the slice: x: 4, y: 4, z: 4, core: 2. Of those that a mesh axis runs over, the one named last changes fastest.
Arguments:
- hidden_in: bfloat16 [768, 4096], P('dp'), may hold values from -6 to 6
- queries: bfloat16 [768, 8192], P('dp', 'tensor'), may hold values from -150 to 150
- key_cache: bfloat16 [768, 4, 768, 128], P('dp', 'tensor'), may hold values from -5 to 5
- cached_value_rows: bfloat16 [768, 4, 768, 128], P('dp', 'tensor'), may hold values from -6 to 6
- cache_lengths: int32 [768], P('dp'), may hold values from 48 to 768, as said below
- out_weight: bfloat16 [8192, 4096], P('tensor', 'dp'), may hold values from -0.0625 to 0.0625
- expert_ids: int32 [768, 8], P('dp'), may hold values from 0 to 127, as said below
- route_probs: float32 [768, 8], P('dp'), may hold values from 0.05 to 1
- w_gate: bfloat16 [128, 4096, 768], P(('dp', 'tensor')), may hold values from -0.09375 to 0.09375
- w_up: bfloat16 [128, 4096, 768], P(('dp', 'tensor')), may hold values from -0.09375 to 0.09375
- w_down: bfloat16 [128, 768, 4096], P(('dp', 'tensor')), may hold values from -0.21875 to 0.21875
Outputs:
- layer_out: bfloat16 [768, 4096], P('dp', 'tensor')
The draws below stay inside these ranges and needn't reach their ends.
Inputs may be any that keep to these rules, and one draw needn't show every extreme that they name: `expert_ids`: each row names 8 different experts; among the rows of one index of dp no expert is named more than 2 times, and one expert is named exactly 2 times in every such group of rows. Row r attends to cache positions 0 to cache_lengths[r] - 1; some row has all 768.
All inputs are finite; a program needn't handle non-finite values.
Results may differ from the reference program's by a relative error of at most 0.01.
Values may be sent and summed in bfloat16 or wider, within the bound.
No kernel may reach another device: no remote copies, remote signals or barrier semaphores. Data moves between devices by JAX's collectives and lax.ppermute only.
A program may use at most 128 MiB of HBM per device.

```python
import math
import jax
import jax.numpy as jnp
from jax import lax

D = 4096
QUERY_HEADS = 64
KEY_VALUE_HEADS = 4
HEAD_SIZE = 128
EXPERTS = 128
TOP = 8
FF = 768
CAP = 2
ROWS_DEV = 24
CACHE_POSITIONS = 768
BATCH_ROWS = 768
N_DP = 32


def draw_queries(key, part):
    value_rows = jnp.clip(jax.random.normal(jax.random.fold_in(key, 21), (BATCH_ROWS, QUERY_HEADS, HEAD_SIZE), jnp.float32), -4.0, 4.0)
    return value_rows.reshape(BATCH_ROWS, QUERY_HEADS * HEAD_SIZE).astype(jnp.bfloat16)


def draw_key_cache(key, part):
    value_rows = jnp.clip(jax.random.normal(jax.random.fold_in(key, 31), (BATCH_ROWS, KEY_VALUE_HEADS, CACHE_POSITIONS, HEAD_SIZE), jnp.float32), -4.0, 4.0)
    return value_rows.astype(jnp.bfloat16)


def draw_cache_lengths(key, part):
    blocks = BATCH_ROWS // ROWS_DEV
    full_block = jax.random.randint(jax.random.fold_in(key, 41), (), 0, blocks)
    caps = jax.random.randint(jax.random.fold_in(key, 42), (blocks,), CACHE_POSITIONS // 4, CACHE_POSITIONS + 1)
    caps = jnp.where(jnp.arange(blocks, dtype=jnp.int32) == full_block, CACHE_POSITIONS, caps)
    row_caps = jnp.repeat(caps, ROWS_DEV)
    lengths = jax.random.randint(jax.random.fold_in(key, 43), (BATCH_ROWS,), CACHE_POSITIONS // 16, row_caps + 1)
    longest = jnp.repeat(jax.random.randint(jax.random.fold_in(key, 44), (blocks,), 0, ROWS_DEV), ROWS_DEV)
    within = jnp.arange(BATCH_ROWS, dtype=jnp.int32) % ROWS_DEV
    return jnp.where(within == longest, row_caps, lengths).astype(jnp.int32)


def draw_expert_ids(key, part):
    blocks = BATCH_ROWS // ROWS_DEV
    total = ROWS_DEV * TOP
    hottest = jax.random.randint(jax.random.fold_in(key, 51), (), 0, EXPERTS)

    def one_block(block_key):
        order = jax.random.permutation(jax.random.fold_in(block_key, 1), EXPERTS).astype(jnp.int32)
        order = jnp.where(order == hottest, order[0], order)
        order = order.at[0].set(hottest)
        doubled = jax.random.randint(jax.random.fold_in(block_key, 2), (), max(1, total - EXPERTS), total // 2 + 1)
        position = jnp.arange(EXPERTS, dtype=jnp.int32)
        counts = jnp.where(position < doubled, 2, jnp.where(position < total - doubled, 1, 0)).astype(jnp.int32)
        ends = jnp.cumsum(counts)
        entry = jnp.searchsorted(ends, jnp.arange(total, dtype=jnp.int32), side='right')
        multiset = order[entry]
        table = multiset.reshape(TOP, ROWS_DEV).T
        shuffle = jax.random.permutation(jax.random.fold_in(block_key, 3), ROWS_DEV)
        return table[shuffle]
    block_keys = jax.random.split(jax.random.fold_in(key, 52), blocks)
    return jax.vmap(one_block)(block_keys).reshape(BATCH_ROWS, TOP).astype(jnp.int32)


def block_levels(own_key, shape, cuts, low, high):
    def one(axis_at, shards_of):
        draws = jax.random.uniform(jax.random.fold_in(jax.random.fold_in(own_key, 6), axis_at), (shards_of,), jnp.float32, low / len(cuts), high / len(cuts))
        return jnp.repeat(jnp.exp(draws), shape[axis_at] // shards_of).reshape((-1,) + (1,) * (len(shape) - axis_at - 1))

    loudness = one(*cuts[0])
    for cut in cuts[1:]:
        loudness = loudness * one(*cut)
    return loudness


def noise(key, shape, scale, most, pieces=(), kind=jnp.bfloat16):
    entries = jax.random.normal(key, shape, jnp.float32) * scale
    if len(pieces) > 0:
        entries = block_levels(key, shape, pieces, -0.22, 0.18) * entries
    return jnp.clip(entries, min=-most, max=most).astype(kind)


def setup_inputs(seed: int = 0) -> dict:
    key_of = jax.random.split(jax.random.key(seed), 12)
    hidden_in = noise(key_of[0], (BATCH_ROWS, D), 1.0, 6.0, ((0, 32),))
    queries = draw_queries(jax.random.fold_in(key_of[11], 71), 0)
    key_cache = draw_key_cache(jax.random.fold_in(key_of[11], 71), 0)
    cached_value_rows = noise(key_of[3], (BATCH_ROWS, KEY_VALUE_HEADS, CACHE_POSITIONS, HEAD_SIZE), 1.0, 6.0, ((0, 32), (1, 4)))
    cache_lengths = draw_cache_lengths(jax.random.fold_in(key_of[11], 71), 0)
    out_weight = noise(key_of[5], (QUERY_HEADS * HEAD_SIZE, D), (QUERY_HEADS * HEAD_SIZE) ** -0.5, 0.0625, ((0, 4), (1, 32)))
    expert_ids = draw_expert_ids(jax.random.fold_in(key_of[11], 71), 0)
    route_probs = jnp.clip(jnp.exp(math.log(1.0) - 2.9957323 * jax.random.uniform(key_of[7], (BATCH_ROWS, TOP), jnp.float32) ** block_levels(key_of[7], (BATCH_ROWS, TOP), ((0, 32),), -0.2, 0.2)), 0.05, 1.0)
    w_gate = noise(key_of[8], (EXPERTS, D, FF), D ** -0.5, 0.09375, ((0, 128),))
    w_up = noise(key_of[9], (EXPERTS, D, FF), D ** -0.5, 0.09375, ((0, 128),))
    w_down = noise(key_of[10], (EXPERTS, FF, D), FF ** -0.5, 0.21875, ((0, 128),))
    return {"hidden_in": hidden_in, "queries": queries, "key_cache": key_cache, "cached_value_rows": cached_value_rows, "cache_lengths": cache_lengths, "out_weight": out_weight, "expert_ids": expert_ids, "route_probs": route_probs, "w_gate": w_gate, "w_up": w_up, "w_down": w_down}


def reference(hidden_in, queries, key_cache, cached_value_rows, cache_lengths, out_weight, expert_ids, route_probs, w_gate, w_up, w_down):
    group_width = QUERY_HEADS // KEY_VALUE_HEADS
    score_scale = 1.0 / math.sqrt(HEAD_SIZE)
    query_head_count = queries.astype(jnp.float32).reshape(BATCH_ROWS, KEY_VALUE_HEADS, group_width, HEAD_SIZE).transpose(1, 0, 2, 3)
    valid_mask = (jnp.arange(CACHE_POSITIONS, dtype=jnp.int32)[None, :] < cache_lengths.astype(jnp.int32)[:, None])[:, None, :]

    def attend(operands):
        query_one, keys_one, values_one = operands
        scores = jnp.einsum('rgd,rld->rgl', query_one, keys_one.astype(jnp.float32)) * score_scale
        scores = jnp.where(valid_mask, scores, -jnp.inf)
        largest = lax.optimization_barrier(jnp.max(scores, axis=-1, keepdims=True))
        exponent = jnp.exp(scores - largest)
        attn_probs = (exponent / lax.optimization_barrier(jnp.sum(exponent, axis=-1, keepdims=True))).astype(jnp.bfloat16)
        return jnp.einsum('rgl,rld->rgd', attn_probs.astype(jnp.float32), values_one.astype(jnp.float32)).astype(jnp.bfloat16)
    heads_out = lax.map(attend, (query_head_count, key_cache.transpose(1, 0, 2, 3), cached_value_rows.transpose(1, 0, 2, 3)))
    attn_out = heads_out.transpose(1, 0, 2, 3).reshape(BATCH_ROWS, QUERY_HEADS * HEAD_SIZE)
    projected = jnp.dot(attn_out, out_weight, preferred_element_type=jnp.float32).astype(jnp.bfloat16)
    residual = (hidden_in.astype(jnp.float32) + projected.astype(jnp.float32)).astype(jnp.bfloat16)
    resid_f = residual.astype(jnp.float32)
    normed = (resid_f * lax.rsqrt(lax.optimization_barrier(jnp.mean(resid_f * resid_f, axis=-1, keepdims=True)) + 1e-06)).astype(jnp.bfloat16)
    route_weights = route_probs / lax.optimization_barrier(jnp.sum(route_probs, axis=-1, keepdims=True))
    slots_all = N_DP * CAP

    def one_expert(mixture, operands):
        gate_one, up_one, down_one, expert = operands
        member = expert_ids == expert
        weight_row = lax.optimization_barrier(jnp.sum(jnp.where(member, route_weights, 0.0), axis=-1))
        chosen = jnp.any(member, axis=-1)
        row_index = jnp.nonzero(chosen, size=slots_all, fill_value=0)[0].astype(jnp.int32)
        live_slot = jnp.arange(slots_all, dtype=jnp.int32) < jnp.sum(chosen.astype(jnp.int32))
        rows_in = normed[row_index]
        gate_proj = jnp.dot(rows_in, gate_one, preferred_element_type=jnp.float32)
        up_proj = jnp.dot(rows_in, up_one, preferred_element_type=jnp.float32)
        activated = (jax.nn.silu(gate_proj) * up_proj).astype(jnp.bfloat16)
        expert_out = jnp.dot(activated, down_one, preferred_element_type=jnp.float32).astype(jnp.bfloat16)
        scaled = jnp.where(live_slot, weight_row[row_index], 0.0)[:, None] * expert_out.astype(jnp.float32)
        return (mixture.at[row_index].add(scaled), None)
    mixture, unused = lax.scan(one_expert, jnp.zeros((BATCH_ROWS, D), jnp.float32), (w_gate, w_up, w_down, jnp.arange(EXPERTS, dtype=jnp.int32)))
    return (resid_f + mixture).astype(jnp.bfloat16)
```

```python
import math

import jax
import jax.numpy as jnp
import numpy as np
from jax import lax
from jax.sharding import Mesh, PartitionSpec as P

CAP = 2
DP = ("x", "z", "c")
ALL = ("x", "z", "c", "tensor")


def residual_norm(hidden_rows, projected):
    residual = (hidden_rows.astype(jnp.float32) + projected.astype(jnp.float32)).astype(
        jnp.bfloat16
    )
    resid_f = residual.astype(jnp.float32)
    normed = (
        resid_f * lax.rsqrt(jnp.mean(resid_f * resid_f, axis=-1, keepdims=True) + 1e-06)
    ).astype(jnp.bfloat16)
    return (residual, normed)


def local(
    hidden_in,
    queries,
    key_cache,
    cached_value_rows,
    cache_lengths,
    out_weight,
    expert_ids,
    route_probs,
    w_gate,
    w_up,
    w_down,
):
    n_xz = lax.axis_size("x") * lax.axis_size("z")
    n_c = lax.axis_size("c")
    dp_count = n_xz * n_c
    tp_count = lax.axis_size("tensor")
    tp_rank = lax.axis_index("tensor")
    c_rank = lax.axis_index("c")
    rows_dev, kv_local, cache_len, head_dim = key_cache.shape
    groups = queries.shape[1] // (kv_local * head_dim)
    model_width = hidden_in.shape[1]
    col_block = model_width // dp_count
    n_all = dp_count * tp_count

    query_head_count = queries.reshape(rows_dev, kv_local, groups, head_dim)
    scores = jnp.einsum(
        "rhgd,rhld->rhgl", query_head_count, key_cache, preferred_element_type=jnp.float32
    ) * (1.0 / math.sqrt(head_dim))
    valid_mask = (jnp.arange(cache_len, dtype=jnp.int32)[None, :] < cache_lengths[:, None])[
        :, None, None, :
    ]
    scores = jnp.where(valid_mask, scores, -jnp.inf)
    largest = jnp.max(scores, axis=-1, keepdims=True)
    exponent = jnp.exp(scores - largest)
    attn_probs = (exponent / jnp.sum(exponent, axis=-1, keepdims=True)).astype(jnp.bfloat16)
    attn_out = jnp.einsum(
        "rhgl,rhld->rhgd", attn_probs, cached_value_rows, preferred_element_type=jnp.float32
    ).astype(jnp.bfloat16)
    attn_out = attn_out.reshape(rows_dev, kv_local * groups * head_dim)

    sent = jnp.broadcast_to(attn_out[None], (n_xz,) + attn_out.shape)
    mine = lax.all_to_all(sent, ("x", "z"), 0, 0, tiled=True)
    other = lax.ppermute(mine, "c", [(i, (i + 1) % n_c) for i in range(n_c)])
    part_mine = jnp.einsum("ird,dc->irc", mine, out_weight, preferred_element_type=jnp.float32)
    part_other = jnp.einsum("ird,dc->irc", other, out_weight, preferred_element_type=jnp.float32)
    slots = jnp.stack([part_mine, part_other], axis=1)
    slots = jnp.where(c_rank == 0, slots, slots[:, ::-1])
    partial_value = slots.reshape(dp_count, rows_dev, col_block).astype(jnp.bfloat16)

    sent = jnp.broadcast_to(partial_value[:, None], (dp_count, tp_count, rows_dev, col_block))
    got = lax.all_to_all(sent.reshape(n_all, rows_dev, col_block), ALL, 0, 0, tiled=True)
    projected = got.reshape(dp_count, tp_count, rows_dev, col_block).astype(jnp.float32).sum(1)
    projected = projected.transpose(1, 0, 2).reshape(rows_dev, model_width).astype(jnp.bfloat16)
    residual, normed = residual_norm(hidden_in, projected)

    exp_dev = w_gate.shape[0]
    n_exp = n_all * exp_dev
    matches = expert_ids[:, :, None] == jnp.arange(n_exp, dtype=jnp.int32)[None, None, :]
    assigned = jnp.sum(matches.astype(jnp.int32), axis=1)
    slot_rank = jnp.cumsum(assigned, axis=0) - assigned
    slot_hit = (slot_rank[:, :, None] == jnp.arange(CAP, dtype=jnp.int32)[None, None, :]) & (
        assigned[:, :, None] > 0
    )
    route_weights = route_probs / jnp.sum(route_probs, axis=-1, keepdims=True)
    all_weight = jnp.sum(jnp.where(matches, route_weights[:, :, None], 0.0), axis=1)

    hit_col = slot_hit.reshape(rows_dev, dp_count, tp_count, exp_dev, CAP)
    hit_col = lax.dynamic_index_in_dim(hit_col, tp_rank, axis=2, keepdims=False)
    outgoing = jnp.einsum(
        "rmjc,rd->mjcd", hit_col.astype(jnp.bfloat16), normed, preferred_element_type=jnp.float32
    ).astype(jnp.bfloat16)
    arrived_slots = lax.all_to_all(outgoing, DP, 0, 0, tiled=True)
    gate_proj = jnp.einsum(
        "sjcd,jdf->sjcf", arrived_slots, w_gate, preferred_element_type=jnp.float32
    )
    up_proj = jnp.einsum("sjcd,jdf->sjcf", arrived_slots, w_up, preferred_element_type=jnp.float32)
    activated = (jax.nn.silu(gate_proj) * up_proj).astype(jnp.bfloat16)
    expert_out = jnp.einsum(
        "sjcf,jfd->sjcd", activated, w_down, preferred_element_type=jnp.float32
    ).astype(jnp.bfloat16)

    width_share = model_width // tp_count
    back = expert_out.reshape(dp_count, exp_dev, CAP, tp_count, width_share)
    back = back.transpose(0, 3, 1, 2, 4).reshape(n_all, exp_dev * CAP, width_share)
    results = lax.all_to_all(back, ALL, 0, 0, tiled=True)
    combine_table = jnp.where(slot_hit, all_weight[:, :, None], 0.0)
    mixture = jnp.einsum(
        "rmc,mcd->rd",
        combine_table,
        results.reshape(n_exp, CAP, width_share).astype(jnp.float32),
        precision=lax.Precision.HIGHEST,
    )
    residual_own = lax.dynamic_slice_in_dim(residual, tp_rank * width_share, width_share, 1)
    return (residual_own.astype(jnp.float32) + mixture).astype(jnp.bfloat16)


def split_mesh(mesh):
    devices = np.asarray(mesh.devices)
    n_dp, n_t = devices.shape
    n_c = 2
    try:
        xs = sorted({d.coords[0] for d in devices.flat})
        n_x = len(xs)
    except Exception:
        n_x = 4
    n_z = n_dp // (n_x * n_c)
    return Mesh(devices.reshape(n_x, n_z, n_c, n_t), ALL)


def solution(mesh):
    fine = split_mesh(mesh)
    placed = (
        P(DP, None),
        P(DP, "tensor"),
        P(DP, "tensor", None, None),
        P(DP, "tensor", None, None),
        P(DP),
        P("tensor", DP),
        P(DP, None),
        P(DP, None),
        P(ALL, None, None),
        P(ALL, None, None),
        P(ALL, None, None),
    )
    return jax.shard_map(
        local, mesh=fine, in_specs=placed, out_specs=P(DP, "tensor"), check_vma=False
    )
```

```python
import math

import jax
import jax.numpy as jnp
import numpy as np
from jax import lax
from jax.experimental import pallas as pl
from jax.experimental.pallas import tpu as pltpu
from jax.sharding import Mesh, PartitionSpec as P

CAP = 2
DP = ("x", "z", "c")
ALL = ("x", "z", "c", "tensor")


def residual_norm(hidden_rows, projected):
    residual = (hidden_rows.astype(jnp.float32) + projected.astype(jnp.float32)).astype(
        jnp.bfloat16
    )
    resid_f = residual.astype(jnp.float32)
    normed = (
        resid_f * lax.rsqrt(jnp.mean(resid_f * resid_f, axis=-1, keepdims=True) + 1e-06)
    ).astype(jnp.bfloat16)
    return (residual, normed)


def ffn_kernel(x_ref, wg_ref, wu_ref, wd_ref, o_ref):
    x = x_ref[...]
    gate = jnp.dot(x, wg_ref[...], preferred_element_type=jnp.float32)
    up = jnp.dot(x, wu_ref[...], preferred_element_type=jnp.float32)
    activated = (gate / (1.0 + jnp.exp(-gate)) * up).astype(jnp.bfloat16)
    o_ref[...] = jnp.dot(activated, wd_ref[...], preferred_element_type=jnp.float32).astype(
        o_ref.dtype
    )


def expert_ffn(x, wg, wu, wd):
    rows, width = x.shape
    ff = wg.shape[1]
    vmem = pl.BlockSpec(memory_space=pltpu.VMEM)
    return pl.pallas_call(
        ffn_kernel,
        out_shape=jax.ShapeDtypeStruct((rows, width), jnp.bfloat16),
        in_specs=[vmem] * 4,
        out_specs=vmem,
        compiler_params=pltpu.CompilerParams(vmem_limit_bytes=56 * 1024 * 1024),
        cost_estimate=pl.CostEstimate(
            flops=6 * rows * width * ff,
            transcendentals=rows * ff,
            bytes_accessed=2 * (3 * width * ff + 2 * rows * width),
        ),
    )(x, wg, wu, wd)


def local(
    hidden_in,
    queries,
    key_cache,
    cached_value_rows,
    cache_lengths,
    out_weight,
    expert_ids,
    route_probs,
    w_gate,
    w_up,
    w_down,
):
    n_xz = lax.axis_size("x") * lax.axis_size("z")
    n_c = lax.axis_size("c")
    dp_count = n_xz * n_c
    tp_count = lax.axis_size("tensor")
    tp_rank = lax.axis_index("tensor")
    c_rank = lax.axis_index("c")
    rows_dev, kv_local, cache_len, head_dim = key_cache.shape
    groups = queries.shape[1] // (kv_local * head_dim)
    model_width = hidden_in.shape[1]
    col_block = model_width // dp_count
    n_all = dp_count * tp_count

    query_head_count = queries.reshape(rows_dev, kv_local, groups, head_dim)
    scores = jnp.einsum(
        "rhgd,rhld->rhgl", query_head_count, key_cache, preferred_element_type=jnp.float32
    ) * (1.0 / math.sqrt(head_dim))
    valid_mask = (jnp.arange(cache_len, dtype=jnp.int32)[None, :] < cache_lengths[:, None])[
        :, None, None, :
    ]
    scores = jnp.where(valid_mask, scores, -jnp.inf)
    largest = jnp.max(scores, axis=-1, keepdims=True)
    exponent = jnp.exp(scores - largest)
    attn_probs = (exponent / jnp.sum(exponent, axis=-1, keepdims=True)).astype(jnp.bfloat16)
    attn_out = jnp.einsum(
        "rhgl,rhld->rhgd", attn_probs, cached_value_rows, preferred_element_type=jnp.float32
    ).astype(jnp.bfloat16)
    attn_out = attn_out.reshape(rows_dev, kv_local * groups * head_dim)

    sent = jnp.broadcast_to(attn_out[None], (n_xz,) + attn_out.shape)
    mine = lax.all_to_all(sent, ("x", "z"), 0, 0, tiled=True)
    other = lax.ppermute(mine, "c", [(i, (i + 1) % n_c) for i in range(n_c)])
    part_mine = jnp.einsum("ird,dc->irc", mine, out_weight, preferred_element_type=jnp.float32)
    part_other = jnp.einsum("ird,dc->irc", other, out_weight, preferred_element_type=jnp.float32)
    slots = jnp.stack([part_mine, part_other], axis=1)
    slots = jnp.where(c_rank == 0, slots, slots[:, ::-1])
    partial_value = slots.reshape(dp_count, rows_dev, col_block).astype(jnp.bfloat16)

    sent = jnp.broadcast_to(partial_value[:, None], (dp_count, tp_count, rows_dev, col_block))
    got = lax.all_to_all(sent.reshape(n_all, rows_dev, col_block), ALL, 0, 0, tiled=True)
    projected = got.reshape(dp_count, tp_count, rows_dev, col_block).astype(jnp.float32).sum(1)
    projected = projected.transpose(1, 0, 2).reshape(rows_dev, model_width).astype(jnp.bfloat16)
    residual, normed = residual_norm(hidden_in, projected)

    exp_dev = w_gate.shape[0]
    n_exp = n_all * exp_dev
    matches = expert_ids[:, :, None] == jnp.arange(n_exp, dtype=jnp.int32)[None, None, :]
    assigned = jnp.sum(matches.astype(jnp.int32), axis=1)
    slot_rank = jnp.cumsum(assigned, axis=0) - assigned
    slot_hit = (slot_rank[:, :, None] == jnp.arange(CAP, dtype=jnp.int32)[None, None, :]) & (
        assigned[:, :, None] > 0
    )
    route_weights = route_probs / jnp.sum(route_probs, axis=-1, keepdims=True)
    all_weight = jnp.sum(jnp.where(matches, route_weights[:, :, None], 0.0), axis=1)

    hit_col = slot_hit.reshape(rows_dev, dp_count, tp_count, exp_dev, CAP)
    hit_col = lax.dynamic_index_in_dim(hit_col, tp_rank, axis=2, keepdims=False)
    outgoing = jnp.einsum(
        "rmjc,rd->mjcd", hit_col.astype(jnp.bfloat16), normed, preferred_element_type=jnp.float32
    ).astype(jnp.bfloat16)
    arrived_slots = lax.all_to_all(outgoing, DP, 0, 0, tiled=True)
    expert_out = jnp.stack(
        [
            expert_ffn(
                arrived_slots[:, j].reshape(dp_count * CAP, model_width), w_gate[j], w_up[j], w_down[j]
            ).reshape(dp_count, CAP, model_width)
            for j in range(exp_dev)
        ],
        axis=1,
    )

    width_share = model_width // tp_count
    back = expert_out.reshape(dp_count, exp_dev, CAP, tp_count, width_share)
    back = back.transpose(0, 3, 1, 2, 4).reshape(n_all, exp_dev * CAP, width_share)
    results = lax.all_to_all(back, ALL, 0, 0, tiled=True)
    combine_table = jnp.where(slot_hit, all_weight[:, :, None], 0.0)
    mixture = jnp.einsum(
        "rmc,mcd->rd",
        combine_table,
        results.reshape(n_exp, CAP, width_share).astype(jnp.float32),
        precision=lax.Precision.HIGHEST,
    )
    residual_own = lax.dynamic_slice_in_dim(residual, tp_rank * width_share, width_share, 1)
    return (residual_own.astype(jnp.float32) + mixture).astype(jnp.bfloat16)


def split_mesh(mesh):
    devices = np.asarray(mesh.devices)
    n_dp, n_t = devices.shape
    n_c = 2
    try:
        xs = sorted({d.coords[0] for d in devices.flat})
        n_x = len(xs)
    except Exception:
        n_x = 4
    n_z = n_dp // (n_x * n_c)
    return Mesh(devices.reshape(n_x, n_z, n_c, n_t), ALL)


def solution(mesh):
    fine = split_mesh(mesh)
    placed = (
        P(DP, None),
        P(DP, "tensor"),
        P(DP, "tensor", None, None),
        P(DP, "tensor", None, None),
        P(DP),
        P("tensor", DP),
        P(DP, None),
        P(DP, None),
        P(ALL, None, None),
        P(ALL, None, None),
        P(ALL, None, None),
    )
    return jax.shard_map(
        local, mesh=fine, in_specs=placed, out_specs=P(DP, "tensor"), check_vma=False
    )
```

```python
import math

import jax
import jax.numpy as jnp
import numpy as np
from jax import lax
from jax.sharding import Mesh, PartitionSpec as P

CAP = 2
DP = ("x", "z", "c")
ALL = ("x", "z", "c", "tensor")


def residual_norm(hidden_rows, projected):
    residual = (hidden_rows.astype(jnp.float32) + projected.astype(jnp.float32)).astype(
        jnp.bfloat16
    )
    resid_f = residual.astype(jnp.float32)
    normed = (
        resid_f * lax.rsqrt(jnp.mean(resid_f * resid_f, axis=-1, keepdims=True) + 1e-06)
    ).astype(jnp.bfloat16)
    return (residual, normed)


def local(
    hidden_in,
    queries,
    key_cache,
    cached_value_rows,
    cache_lengths,
    out_weight,
    expert_ids,
    route_probs,
    w_gate,
    w_up,
    w_down,
):
    n_xz = lax.axis_size("x") * lax.axis_size("z")
    n_c = lax.axis_size("c")
    dp_count = n_xz * n_c
    tp_count = lax.axis_size("tensor")
    tp_rank = lax.axis_index("tensor")
    c_rank = lax.axis_index("c")
    rows_dev, kv_local, cache_len, head_dim = key_cache.shape
    groups = queries.shape[1] // (kv_local * head_dim)
    model_width = hidden_in.shape[1]
    col_block = model_width // dp_count
    n_all = dp_count * tp_count

    query_head_count = queries.reshape(rows_dev, kv_local, groups, head_dim)
    valid_mask = (jnp.arange(cache_len, dtype=jnp.int32)[None, :] < cache_lengths[:, None])[
        :, None, None, :
    ]
    n_chunks = 2
    per_chunk = groups // n_chunks
    weight_rows = out_weight.reshape(kv_local, groups, head_dim, col_block)
    partial_f = None
    for k in range(n_chunks):
        q_k = query_head_count[:, :, k * per_chunk : (k + 1) * per_chunk]
        scores = jnp.einsum(
            "rhgd,rhld->rhgl", q_k, key_cache, preferred_element_type=jnp.float32
        ) * (1.0 / math.sqrt(head_dim))
        scores = jnp.where(valid_mask, scores, -jnp.inf)
        largest = jnp.max(scores, axis=-1, keepdims=True)
        exponent = jnp.exp(scores - largest)
        attn_probs = (exponent / jnp.sum(exponent, axis=-1, keepdims=True)).astype(jnp.bfloat16)
        attn_out = jnp.einsum(
            "rhgl,rhld->rhgd", attn_probs, cached_value_rows, preferred_element_type=jnp.float32
        ).astype(jnp.bfloat16)
        attn_out = attn_out.reshape(rows_dev, kv_local * per_chunk * head_dim)
        w_k = weight_rows[:, k * per_chunk : (k + 1) * per_chunk].reshape(-1, col_block)
        sent = jnp.broadcast_to(attn_out[None], (n_xz,) + attn_out.shape)
        mine = lax.all_to_all(sent, ("x", "z"), 0, 0, tiled=True)
        other = lax.ppermute(mine, "c", [(i, (i + 1) % n_c) for i in range(n_c)])
        part_mine = jnp.einsum("ird,dc->irc", mine, w_k, preferred_element_type=jnp.float32)
        part_other = jnp.einsum("ird,dc->irc", other, w_k, preferred_element_type=jnp.float32)
        part = jnp.stack([part_mine, part_other], axis=1)
        partial_f = part if partial_f is None else partial_f + part
    slots = jnp.where(c_rank == 0, partial_f, partial_f[:, ::-1])
    partial_value = slots.reshape(dp_count, rows_dev, col_block).astype(jnp.bfloat16)

    sent = jnp.broadcast_to(partial_value[:, None], (dp_count, tp_count, rows_dev, col_block))
    got = lax.all_to_all(sent.reshape(n_all, rows_dev, col_block), ALL, 0, 0, tiled=True)
    projected = got.reshape(dp_count, tp_count, rows_dev, col_block).astype(jnp.float32).sum(1)
    projected = projected.transpose(1, 0, 2).reshape(rows_dev, model_width).astype(jnp.bfloat16)
    residual, normed = residual_norm(hidden_in, projected)

    exp_dev = w_gate.shape[0]
    n_exp = n_all * exp_dev
    matches = expert_ids[:, :, None] == jnp.arange(n_exp, dtype=jnp.int32)[None, None, :]
    assigned = jnp.sum(matches.astype(jnp.int32), axis=1)
    slot_rank = jnp.cumsum(assigned, axis=0) - assigned
    slot_hit = (slot_rank[:, :, None] == jnp.arange(CAP, dtype=jnp.int32)[None, None, :]) & (
        assigned[:, :, None] > 0
    )
    route_weights = route_probs / jnp.sum(route_probs, axis=-1, keepdims=True)
    all_weight = jnp.sum(jnp.where(matches, route_weights[:, :, None], 0.0), axis=1)

    hit_col = slot_hit.reshape(rows_dev, dp_count, tp_count, exp_dev, CAP)
    hit_col = lax.dynamic_index_in_dim(hit_col, tp_rank, axis=2, keepdims=False)
    outgoing = jnp.einsum(
        "rmjc,rd->mjcd", hit_col.astype(jnp.bfloat16), normed, preferred_element_type=jnp.float32
    ).astype(jnp.bfloat16)
    arrived_slots = lax.all_to_all(outgoing, DP, 0, 0, tiled=True)
    gate_proj = jnp.einsum(
        "sjcd,jdf->sjcf", arrived_slots, w_gate, preferred_element_type=jnp.float32
    )
    up_proj = jnp.einsum("sjcd,jdf->sjcf", arrived_slots, w_up, preferred_element_type=jnp.float32)
    activated = (jax.nn.silu(gate_proj) * up_proj).astype(jnp.bfloat16)
    expert_out = jnp.einsum(
        "sjcf,jfd->sjcd", activated, w_down, preferred_element_type=jnp.float32
    ).astype(jnp.bfloat16)

    width_share = model_width // tp_count
    back = expert_out.reshape(dp_count, exp_dev, CAP, tp_count, width_share)
    back = back.transpose(0, 3, 1, 2, 4).reshape(n_all, exp_dev * CAP, width_share)
    results = lax.all_to_all(back, ALL, 0, 0, tiled=True)
    combine_table = jnp.where(slot_hit, all_weight[:, :, None], 0.0)
    mixture = jnp.einsum(
        "rmc,mcd->rd",
        combine_table,
        results.reshape(n_exp, CAP, width_share).astype(jnp.float32),
        precision=lax.Precision.HIGHEST,
    )
    residual_own = lax.dynamic_slice_in_dim(residual, tp_rank * width_share, width_share, 1)
    return (residual_own.astype(jnp.float32) + mixture).astype(jnp.bfloat16)


def split_mesh(mesh):
    devices = np.asarray(mesh.devices)
    n_dp, n_t = devices.shape
    n_c = 2
    try:
        xs = sorted({d.coords[0] for d in devices.flat})
        n_x = len(xs)
    except Exception:
        n_x = 4
    n_z = n_dp // (n_x * n_c)
    return Mesh(devices.reshape(n_x, n_z, n_c, n_t), ALL)


def solution(mesh):
    fine = split_mesh(mesh)
    placed = (
        P(DP, None),
        P(DP, "tensor"),
        P(DP, "tensor", None, None),
        P(DP, "tensor", None, None),
        P(DP),
        P("tensor", DP),
        P(DP, None),
        P(DP, None),
        P(ALL, None, None),
        P(ALL, None, None),
        P(ALL, None, None),
    )
    return jax.shard_map(
        local, mesh=fine, in_specs=placed, out_specs=P(DP, "tensor"), check_vma=False
    )
```

```python
import functools
import math

import jax
import jax.numpy as jnp
import numpy as np
from jax import lax
from jax.experimental import pallas as pl
from jax.experimental.pallas import tpu as pltpu
from jax.sharding import Mesh, PartitionSpec as P

CAP = 2
DP = ("x", "z", "c")
ALL = ("x", "z", "c", "tensor")


def residual_norm(hidden_rows, projected):
    residual = (hidden_rows.astype(jnp.float32) + projected.astype(jnp.float32)).astype(
        jnp.bfloat16
    )
    resid_f = residual.astype(jnp.float32)
    normed = (
        resid_f * lax.rsqrt(jnp.mean(resid_f * resid_f, axis=-1, keepdims=True) + 1e-06)
    ).astype(jnp.bfloat16)
    return (residual, normed)


def attention_kernel(len_ref, q_ref, k_ref, v_ref, o_ref, *, block_rows, scale):
    base = pl.program_id(0) * block_rows
    for r in range(block_rows):
        q = q_ref[r]
        k = k_ref[r, 0]
        v = v_ref[r, 0]
        scores = (
            lax.dot_general(q, k, (((1,), (1,)), ((), ())), preferred_element_type=jnp.float32)
            * scale
        )
        position = lax.broadcasted_iota(jnp.int32, scores.shape, 1)
        scores = jnp.where(position < len_ref[base + r], scores, -jnp.inf)
        largest = jnp.max(scores, axis=-1, keepdims=True)
        exponent = jnp.exp(scores - largest)
        probs = (exponent / jnp.sum(exponent, axis=-1, keepdims=True)).astype(jnp.bfloat16)
        o_ref[r] = jnp.dot(probs, v, preferred_element_type=jnp.float32).astype(o_ref.dtype)


def attention(queries, key_cache, cached_value_rows, cache_lengths, block_rows=4):
    rows, kv_local, cache_len, head_dim = key_cache.shape
    assert kv_local == 1
    heads = queries.shape[1] // head_dim
    q = queries.reshape(rows, heads, head_dim)
    kernel = functools.partial(
        attention_kernel, block_rows=block_rows, scale=1.0 / math.sqrt(head_dim)
    )
    grid_spec = pltpu.PrefetchScalarGridSpec(
        num_scalar_prefetch=1,
        grid=(rows // block_rows,),
        in_specs=[
            pl.BlockSpec((block_rows, heads, head_dim), lambda i, n: (i, 0, 0)),
            pl.BlockSpec((block_rows, 1, cache_len, head_dim), lambda i, n: (i, 0, 0, 0)),
            pl.BlockSpec((block_rows, 1, cache_len, head_dim), lambda i, n: (i, 0, 0, 0)),
        ],
        out_specs=pl.BlockSpec((block_rows, heads, head_dim), lambda i, n: (i, 0, 0)),
    )
    out = pl.pallas_call(
        kernel,
        grid_spec=grid_spec,
        out_shape=jax.ShapeDtypeStruct((rows, heads, head_dim), jnp.bfloat16),
        cost_estimate=pl.CostEstimate(
            flops=4 * rows * heads * cache_len * head_dim,
            transcendentals=rows * heads * cache_len,
            bytes_accessed=2 * (2 * rows * cache_len * head_dim + 2 * rows * heads * head_dim),
        ),
    )(cache_lengths, q, key_cache, cached_value_rows)
    return out.reshape(rows, heads * head_dim)


def local(
    hidden_in,
    queries,
    key_cache,
    cached_value_rows,
    cache_lengths,
    out_weight,
    expert_ids,
    route_probs,
    w_gate,
    w_up,
    w_down,
):
    n_xz = lax.axis_size("x") * lax.axis_size("z")
    n_c = lax.axis_size("c")
    dp_count = n_xz * n_c
    tp_count = lax.axis_size("tensor")
    tp_rank = lax.axis_index("tensor")
    c_rank = lax.axis_index("c")
    rows_dev, kv_local, cache_len, head_dim = key_cache.shape
    groups = queries.shape[1] // (kv_local * head_dim)
    model_width = hidden_in.shape[1]
    col_block = model_width // dp_count
    n_all = dp_count * tp_count

    attn_out = attention(queries, key_cache, cached_value_rows, cache_lengths)

    sent = jnp.broadcast_to(attn_out[None], (n_xz,) + attn_out.shape)
    mine = lax.all_to_all(sent, ("x", "z"), 0, 0, tiled=True)
    other = lax.ppermute(mine, "c", [(i, (i + 1) % n_c) for i in range(n_c)])
    part_mine = jnp.einsum("ird,dc->irc", mine, out_weight, preferred_element_type=jnp.float32)
    part_other = jnp.einsum("ird,dc->irc", other, out_weight, preferred_element_type=jnp.float32)
    slots = jnp.stack([part_mine, part_other], axis=1)
    slots = jnp.where(c_rank == 0, slots, slots[:, ::-1])
    partial_value = slots.reshape(dp_count, rows_dev, col_block).astype(jnp.bfloat16)

    sent = jnp.broadcast_to(partial_value[:, None], (dp_count, tp_count, rows_dev, col_block))
    got = lax.all_to_all(sent.reshape(n_all, rows_dev, col_block), ALL, 0, 0, tiled=True)
    projected = got.reshape(dp_count, tp_count, rows_dev, col_block).astype(jnp.float32).sum(1)
    projected = projected.transpose(1, 0, 2).reshape(rows_dev, model_width).astype(jnp.bfloat16)
    residual, normed = residual_norm(hidden_in, projected)

    exp_dev = w_gate.shape[0]
    n_exp = n_all * exp_dev
    matches = expert_ids[:, :, None] == jnp.arange(n_exp, dtype=jnp.int32)[None, None, :]
    assigned = jnp.sum(matches.astype(jnp.int32), axis=1)
    slot_rank = jnp.cumsum(assigned, axis=0) - assigned
    slot_hit = (slot_rank[:, :, None] == jnp.arange(CAP, dtype=jnp.int32)[None, None, :]) & (
        assigned[:, :, None] > 0
    )
    route_weights = route_probs / jnp.sum(route_probs, axis=-1, keepdims=True)
    all_weight = jnp.sum(jnp.where(matches, route_weights[:, :, None], 0.0), axis=1)

    hit_col = slot_hit.reshape(rows_dev, dp_count, tp_count, exp_dev, CAP)
    hit_col = lax.dynamic_index_in_dim(hit_col, tp_rank, axis=2, keepdims=False)
    outgoing = jnp.einsum(
        "rmjc,rd->mjcd", hit_col.astype(jnp.bfloat16), normed, preferred_element_type=jnp.float32
    ).astype(jnp.bfloat16)
    arrived_slots = lax.all_to_all(outgoing, DP, 0, 0, tiled=True)
    gate_proj = jnp.einsum(
        "sjcd,jdf->sjcf", arrived_slots, w_gate, preferred_element_type=jnp.float32
    )
    up_proj = jnp.einsum("sjcd,jdf->sjcf", arrived_slots, w_up, preferred_element_type=jnp.float32)
    activated = (jax.nn.silu(gate_proj) * up_proj).astype(jnp.bfloat16)
    expert_out = jnp.einsum(
        "sjcf,jfd->sjcd", activated, w_down, preferred_element_type=jnp.float32
    ).astype(jnp.bfloat16)

    width_share = model_width // tp_count
    back = expert_out.reshape(dp_count, exp_dev, CAP, tp_count, width_share)
    back = back.transpose(0, 3, 1, 2, 4).reshape(n_all, exp_dev * CAP, width_share)
    results = lax.all_to_all(back, ALL, 0, 0, tiled=True)
    combine_table = jnp.where(slot_hit, all_weight[:, :, None], 0.0)
    mixture = jnp.einsum(
        "rmc,mcd->rd",
        combine_table,
        results.reshape(n_exp, CAP, width_share).astype(jnp.float32),
        precision=lax.Precision.HIGHEST,
    )
    residual_own = lax.dynamic_slice_in_dim(residual, tp_rank * width_share, width_share, 1)
    return (residual_own.astype(jnp.float32) + mixture).astype(jnp.bfloat16)


def split_mesh(mesh):
    devices = np.asarray(mesh.devices)
    n_dp, n_t = devices.shape
    n_c = 2
    try:
        xs = sorted({d.coords[0] for d in devices.flat})
        n_x = len(xs)
    except Exception:
        n_x = 4
    n_z = n_dp // (n_x * n_c)
    return Mesh(devices.reshape(n_x, n_z, n_c, n_t), ALL)


def solution(mesh):
    fine = split_mesh(mesh)
    placed = (
        P(DP, None),
        P(DP, "tensor"),
        P(DP, "tensor", None, None),
        P(DP, "tensor", None, None),
        P(DP),
        P("tensor", DP),
        P(DP, None),
        P(DP, None),
        P(ALL, None, None),
        P(ALL, None, None),
        P(ALL, None, None),
    )
    return jax.shard_map(
        local, mesh=fine, in_specs=placed, out_specs=P(DP, "tensor"), check_vma=False
    )
```

```python
import math

import jax
import jax.numpy as jnp
import numpy as np
from jax import lax
from jax.experimental import pallas as pl
from jax.experimental.pallas import tpu as pltpu
from jax.sharding import Mesh, PartitionSpec as P

CAP = 2
DP = ("x", "z", "c")
ALL = ("x", "z", "c", "tensor")


def residual_norm(hidden_rows, projected):
    residual = (hidden_rows.astype(jnp.float32) + projected.astype(jnp.float32)).astype(
        jnp.bfloat16
    )
    resid_f = residual.astype(jnp.float32)
    normed = (
        resid_f * lax.rsqrt(jnp.mean(resid_f * resid_f, axis=-1, keepdims=True) + 1e-06)
    ).astype(jnp.bfloat16)
    return (residual, normed)


def ffn_kernel(x_ref, wg_ref, wu_ref, wd_ref, o_ref, acc_ref):
    step = pl.program_id(0)

    @pl.when(step == 0)
    def _():
        acc_ref[...] = jnp.zeros_like(acc_ref)

    x = x_ref[...]
    gate = jnp.dot(x, wg_ref[...], preferred_element_type=jnp.float32)
    up = jnp.dot(x, wu_ref[...], preferred_element_type=jnp.float32)
    activated = (gate / (1.0 + jnp.exp(-gate)) * up).astype(jnp.bfloat16)
    acc_ref[...] += jnp.dot(activated, wd_ref[...], preferred_element_type=jnp.float32)

    @pl.when(step == pl.num_programs(0) - 1)
    def _():
        o_ref[...] = acc_ref[...].astype(o_ref.dtype)


def expert_ffn(x, wg, wu, wd, chunk=128):
    rows, width = x.shape
    ff = wg.shape[1]
    return pl.pallas_call(
        ffn_kernel,
        grid=(ff // chunk,),
        in_specs=[
            pl.BlockSpec((rows, width), lambda f: (0, 0)),
            pl.BlockSpec((width, chunk), lambda f: (0, f)),
            pl.BlockSpec((width, chunk), lambda f: (0, f)),
            pl.BlockSpec((chunk, width), lambda f: (f, 0)),
        ],
        out_specs=pl.BlockSpec((rows, width), lambda f: (0, 0)),
        out_shape=jax.ShapeDtypeStruct((rows, width), jnp.bfloat16),
        scratch_shapes=[pltpu.VMEM((rows, width), jnp.float32)],
        compiler_params=pltpu.CompilerParams(vmem_limit_bytes=40 * 1024 * 1024),
        cost_estimate=pl.CostEstimate(
            flops=6 * rows * width * ff,
            transcendentals=rows * ff,
            bytes_accessed=2 * (3 * width * ff + 2 * rows * width),
        ),
    )(x, wg, wu, wd)


def local(
    hidden_in,
    queries,
    key_cache,
    cached_value_rows,
    cache_lengths,
    out_weight,
    expert_ids,
    route_probs,
    w_gate,
    w_up,
    w_down,
):
    n_xz = lax.axis_size("x") * lax.axis_size("z")
    n_c = lax.axis_size("c")
    dp_count = n_xz * n_c
    tp_count = lax.axis_size("tensor")
    tp_rank = lax.axis_index("tensor")
    c_rank = lax.axis_index("c")
    rows_dev, kv_local, cache_len, head_dim = key_cache.shape
    groups = queries.shape[1] // (kv_local * head_dim)
    model_width = hidden_in.shape[1]
    col_block = model_width // dp_count
    n_all = dp_count * tp_count

    query_head_count = queries.reshape(rows_dev, kv_local, groups, head_dim)
    scores = jnp.einsum(
        "rhgd,rhld->rhgl", query_head_count, key_cache, preferred_element_type=jnp.float32
    ) * (1.0 / math.sqrt(head_dim))
    valid_mask = (jnp.arange(cache_len, dtype=jnp.int32)[None, :] < cache_lengths[:, None])[
        :, None, None, :
    ]
    scores = jnp.where(valid_mask, scores, -jnp.inf)
    largest = jnp.max(scores, axis=-1, keepdims=True)
    exponent = jnp.exp(scores - largest)
    attn_probs = (exponent / jnp.sum(exponent, axis=-1, keepdims=True)).astype(jnp.bfloat16)
    attn_out = jnp.einsum(
        "rhgl,rhld->rhgd", attn_probs, cached_value_rows, preferred_element_type=jnp.float32
    ).astype(jnp.bfloat16)
    attn_out = attn_out.reshape(rows_dev, kv_local * groups * head_dim)

    sent = jnp.broadcast_to(attn_out[None], (n_xz,) + attn_out.shape)
    mine = lax.all_to_all(sent, ("x", "z"), 0, 0, tiled=True)
    other = lax.ppermute(mine, "c", [(i, (i + 1) % n_c) for i in range(n_c)])
    part_mine = jnp.einsum("ird,dc->irc", mine, out_weight, preferred_element_type=jnp.float32)
    part_other = jnp.einsum("ird,dc->irc", other, out_weight, preferred_element_type=jnp.float32)
    slots = jnp.stack([part_mine, part_other], axis=1)
    slots = jnp.where(c_rank == 0, slots, slots[:, ::-1])
    partial_value = slots.reshape(dp_count, rows_dev, col_block).astype(jnp.bfloat16)

    sent = jnp.broadcast_to(partial_value[:, None], (dp_count, tp_count, rows_dev, col_block))
    got = lax.all_to_all(sent.reshape(n_all, rows_dev, col_block), ALL, 0, 0, tiled=True)
    projected = got.reshape(dp_count, tp_count, rows_dev, col_block).astype(jnp.float32).sum(1)
    projected = projected.transpose(1, 0, 2).reshape(rows_dev, model_width).astype(jnp.bfloat16)
    residual, normed = residual_norm(hidden_in, projected)

    exp_dev = w_gate.shape[0]
    n_exp = n_all * exp_dev
    matches = expert_ids[:, :, None] == jnp.arange(n_exp, dtype=jnp.int32)[None, None, :]
    assigned = jnp.sum(matches.astype(jnp.int32), axis=1)
    slot_rank = jnp.cumsum(assigned, axis=0) - assigned
    slot_hit = (slot_rank[:, :, None] == jnp.arange(CAP, dtype=jnp.int32)[None, None, :]) & (
        assigned[:, :, None] > 0
    )
    route_weights = route_probs / jnp.sum(route_probs, axis=-1, keepdims=True)
    all_weight = jnp.sum(jnp.where(matches, route_weights[:, :, None], 0.0), axis=1)

    hit_col = slot_hit.reshape(rows_dev, dp_count, tp_count, exp_dev, CAP)
    hit_col = lax.dynamic_index_in_dim(hit_col, tp_rank, axis=2, keepdims=False)
    outgoing = jnp.einsum(
        "rmjc,rd->mjcd", hit_col.astype(jnp.bfloat16), normed, preferred_element_type=jnp.float32
    ).astype(jnp.bfloat16)
    arrived_slots = lax.all_to_all(outgoing, DP, 0, 0, tiled=True)
    assert exp_dev == 1
    expert_out = expert_ffn(
        arrived_slots.reshape(dp_count * CAP, model_width), w_gate[0], w_up[0], w_down[0]
    ).reshape(dp_count, exp_dev, CAP, model_width)

    width_share = model_width // tp_count
    back = expert_out.reshape(dp_count, exp_dev, CAP, tp_count, width_share)
    back = back.transpose(0, 3, 1, 2, 4).reshape(n_all, exp_dev * CAP, width_share)
    results = lax.all_to_all(back, ALL, 0, 0, tiled=True)
    combine_table = jnp.where(slot_hit, all_weight[:, :, None], 0.0)
    mixture = jnp.einsum(
        "rmc,mcd->rd",
        combine_table,
        results.reshape(n_exp, CAP, width_share).astype(jnp.float32),
        precision=lax.Precision.HIGHEST,
    )
    residual_own = lax.dynamic_slice_in_dim(residual, tp_rank * width_share, width_share, 1)
    return (residual_own.astype(jnp.float32) + mixture).astype(jnp.bfloat16)


def split_mesh(mesh):
    devices = np.asarray(mesh.devices)
    n_dp, n_t = devices.shape
    n_c = 2
    try:
        xs = sorted({d.coords[0] for d in devices.flat})
        n_x = len(xs)
    except Exception:
        n_x = 4
    n_z = n_dp // (n_x * n_c)
    return Mesh(devices.reshape(n_x, n_z, n_c, n_t), ALL)


def solution(mesh):
    fine = split_mesh(mesh)
    placed = (
        P(DP, None),
        P(DP, "tensor"),
        P(DP, "tensor", None, None),
        P(DP, "tensor", None, None),
        P(DP),
        P("tensor", DP),
        P(DP, None),
        P(DP, None),
        P(ALL, None, None),
        P(ALL, None, None),
        P(ALL, None, None),
    )
    return jax.shard_map(
        local, mesh=fine, in_specs=placed, out_specs=P(DP, "tensor"), check_vma=False
    )
```

```python
import math

import jax
import jax.numpy as jnp
import numpy as np
from jax import lax
from jax.experimental import pallas as pl
from jax.experimental.pallas import tpu as pltpu
from jax.sharding import Mesh, PartitionSpec as P

CAP = 2
DP = ("x", "z", "c")
ALL = ("x", "z", "c", "tensor")


def residual_norm(hidden_rows, projected):
    residual = (hidden_rows.astype(jnp.float32) + projected.astype(jnp.float32)).astype(
        jnp.bfloat16
    )
    resid_f = residual.astype(jnp.float32)
    normed = (
        resid_f * lax.rsqrt(jnp.mean(resid_f * resid_f, axis=-1, keepdims=True) + 1e-06)
    ).astype(jnp.bfloat16)
    return (residual, normed)


def ffn_kernel(x_ref, wg_ref, wu_ref, wd_ref, o_ref, acc_ref):
    step = pl.program_id(0)

    @pl.when(step == 0)
    def _():
        acc_ref[...] = jnp.zeros_like(acc_ref)

    x = x_ref[...]
    gate = jnp.dot(x, wg_ref[...], preferred_element_type=jnp.float32)
    up = jnp.dot(x, wu_ref[...], preferred_element_type=jnp.float32)
    activated = (gate / (1.0 + jnp.exp(-gate)) * up).astype(jnp.bfloat16)
    acc_ref[...] += jnp.dot(activated, wd_ref[...], preferred_element_type=jnp.float32)

    @pl.when(step == pl.num_programs(0) - 1)
    def _():
        o_ref[...] = acc_ref[...].astype(o_ref.dtype)


def expert_ffn(x, wg, wu, wd, chunk=256):
    rows, width = x.shape
    ff = wg.shape[1]
    return pl.pallas_call(
        ffn_kernel,
        grid=(ff // chunk,),
        in_specs=[
            pl.BlockSpec((rows, width), lambda f: (0, 0)),
            pl.BlockSpec((width, chunk), lambda f: (0, f)),
            pl.BlockSpec((width, chunk), lambda f: (0, f)),
            pl.BlockSpec((chunk, width), lambda f: (f, 0)),
        ],
        out_specs=pl.BlockSpec((rows, width), lambda f: (0, 0)),
        out_shape=jax.ShapeDtypeStruct((rows, width), jnp.bfloat16),
        scratch_shapes=[pltpu.VMEM((rows, width), jnp.float32)],
        compiler_params=pltpu.CompilerParams(vmem_limit_bytes=60 * 1024 * 1024),
        cost_estimate=pl.CostEstimate(
            flops=6 * rows * width * ff,
            transcendentals=rows * ff,
            bytes_accessed=2 * (3 * width * ff + 2 * rows * width),
        ),
    )(x, wg, wu, wd)


def local(
    hidden_in,
    queries,
    key_cache,
    cached_value_rows,
    cache_lengths,
    out_weight,
    expert_ids,
    route_probs,
    w_gate,
    w_up,
    w_down,
):
    n_xz = lax.axis_size("x") * lax.axis_size("z")
    n_c = lax.axis_size("c")
    dp_count = n_xz * n_c
    tp_count = lax.axis_size("tensor")
    tp_rank = lax.axis_index("tensor")
    c_rank = lax.axis_index("c")
    rows_dev, kv_local, cache_len, head_dim = key_cache.shape
    groups = queries.shape[1] // (kv_local * head_dim)
    model_width = hidden_in.shape[1]
    col_block = model_width // dp_count
    n_all = dp_count * tp_count

    query_head_count = queries.reshape(rows_dev, kv_local, groups, head_dim)
    scores = jnp.einsum(
        "rhgd,rhld->rhgl", query_head_count, key_cache, preferred_element_type=jnp.float32
    ) * (1.0 / math.sqrt(head_dim))
    valid_mask = (jnp.arange(cache_len, dtype=jnp.int32)[None, :] < cache_lengths[:, None])[
        :, None, None, :
    ]
    scores = jnp.where(valid_mask, scores, -jnp.inf)
    largest = jnp.max(scores, axis=-1, keepdims=True)
    exponent = jnp.exp(scores - largest)
    attn_probs = (exponent / jnp.sum(exponent, axis=-1, keepdims=True)).astype(jnp.bfloat16)
    attn_out = jnp.einsum(
        "rhgl,rhld->rhgd", attn_probs, cached_value_rows, preferred_element_type=jnp.float32
    ).astype(jnp.bfloat16)
    attn_out = attn_out.reshape(rows_dev, kv_local * groups * head_dim)

    sent = jnp.broadcast_to(attn_out[None], (n_xz,) + attn_out.shape)
    mine = lax.all_to_all(sent, ("x", "z"), 0, 0, tiled=True)
    other = lax.ppermute(mine, "c", [(i, (i + 1) % n_c) for i in range(n_c)])
    part_mine = jnp.einsum("ird,dc->irc", mine, out_weight, preferred_element_type=jnp.float32)
    part_other = jnp.einsum("ird,dc->irc", other, out_weight, preferred_element_type=jnp.float32)
    slots = jnp.stack([part_mine, part_other], axis=1)
    slots = jnp.where(c_rank == 0, slots, slots[:, ::-1])
    partial_value = slots.reshape(dp_count, rows_dev, col_block).astype(jnp.bfloat16)

    sent = jnp.broadcast_to(partial_value[:, None], (dp_count, tp_count, rows_dev, col_block))
    got = lax.all_to_all(sent.reshape(n_all, rows_dev, col_block), ALL, 0, 0, tiled=True)
    projected = got.reshape(dp_count, tp_count, rows_dev, col_block).astype(jnp.float32).sum(1)
    projected = projected.transpose(1, 0, 2).reshape(rows_dev, model_width).astype(jnp.bfloat16)
    residual, normed = residual_norm(hidden_in, projected)

    exp_dev = w_gate.shape[0]
    n_exp = n_all * exp_dev
    matches = expert_ids[:, :, None] == jnp.arange(n_exp, dtype=jnp.int32)[None, None, :]
    assigned = jnp.sum(matches.astype(jnp.int32), axis=1)
    slot_rank = jnp.cumsum(assigned, axis=0) - assigned
    slot_hit = (slot_rank[:, :, None] == jnp.arange(CAP, dtype=jnp.int32)[None, None, :]) & (
        assigned[:, :, None] > 0
    )
    route_weights = route_probs / jnp.sum(route_probs, axis=-1, keepdims=True)
    all_weight = jnp.sum(jnp.where(matches, route_weights[:, :, None], 0.0), axis=1)

    hit_col = slot_hit.reshape(rows_dev, dp_count, tp_count, exp_dev, CAP)
    hit_col = lax.dynamic_index_in_dim(hit_col, tp_rank, axis=2, keepdims=False)
    outgoing = jnp.einsum(
        "rmjc,rd->mjcd", hit_col.astype(jnp.bfloat16), normed, preferred_element_type=jnp.float32
    ).astype(jnp.bfloat16)
    arrived_slots = lax.all_to_all(outgoing, DP, 0, 0, tiled=True)
    assert exp_dev == 1
    expert_out = expert_ffn(
        arrived_slots.reshape(dp_count * CAP, model_width), w_gate[0], w_up[0], w_down[0]
    ).reshape(dp_count, exp_dev, CAP, model_width)

    width_share = model_width // tp_count
    back = expert_out.reshape(dp_count, exp_dev, CAP, tp_count, width_share)
    back = back.transpose(0, 3, 1, 2, 4).reshape(n_all, exp_dev * CAP, width_share)
    results = lax.all_to_all(back, ALL, 0, 0, tiled=True)
    combine_table = jnp.where(slot_hit, all_weight[:, :, None], 0.0)
    mixture = jnp.einsum(
        "rmc,mcd->rd",
        combine_table,
        results.reshape(n_exp, CAP, width_share).astype(jnp.float32),
        precision=lax.Precision.HIGHEST,
    )
    residual_own = lax.dynamic_slice_in_dim(residual, tp_rank * width_share, width_share, 1)
    return (residual_own.astype(jnp.float32) + mixture).astype(jnp.bfloat16)


def split_mesh(mesh):
    devices = np.asarray(mesh.devices)
    n_dp, n_t = devices.shape
    n_c = 2
    try:
        xs = sorted({d.coords[0] for d in devices.flat})
        n_x = len(xs)
    except Exception:
        n_x = 4
    n_z = n_dp // (n_x * n_c)
    return Mesh(devices.reshape(n_x, n_z, n_c, n_t), ALL)


def solution(mesh):
    fine = split_mesh(mesh)
    placed = (
        P(DP, None),
        P(DP, "tensor"),
        P(DP, "tensor", None, None),
        P(DP, "tensor", None, None),
        P(DP),
        P("tensor", DP),
        P(DP, None),
        P(DP, None),
        P(ALL, None, None),
        P(ALL, None, None),
        P(ALL, None, None),
    )
    return jax.shard_map(
        local, mesh=fine, in_specs=placed, out_specs=P(DP, "tensor"), check_vma=False
    )
```

```python
import math

import jax
import jax.numpy as jnp
import numpy as np
from jax import lax
from jax.sharding import Mesh, PartitionSpec as P

CAP = 2
DP = ("x", "z", "c")
ALL = ("x", "z", "c", "tensor")


def residual_norm(hidden_rows, projected):
    residual = (hidden_rows.astype(jnp.float32) + projected.astype(jnp.float32)).astype(
        jnp.bfloat16
    )
    resid_f = residual.astype(jnp.float32)
    normed = (
        resid_f * lax.rsqrt(jnp.mean(resid_f * resid_f, axis=-1, keepdims=True) + 1e-06)
    ).astype(jnp.bfloat16)
    return (residual, normed)


def local(
    hidden_in,
    queries,
    key_cache,
    cached_value_rows,
    cache_lengths,
    out_weight,
    expert_ids,
    route_probs,
    w_gate,
    w_up,
    w_down,
):
    n_xz = lax.axis_size("x") * lax.axis_size("z")
    n_c = lax.axis_size("c")
    dp_count = n_xz * n_c
    tp_count = lax.axis_size("tensor")
    tp_rank = lax.axis_index("tensor")
    c_rank = lax.axis_index("c")
    rows_dev, kv_local, cache_len, head_dim = key_cache.shape
    groups = queries.shape[1] // (kv_local * head_dim)
    model_width = hidden_in.shape[1]
    col_block = model_width // dp_count
    n_all = dp_count * tp_count

    query_head_count = queries.reshape(rows_dev, kv_local, groups, head_dim)
    scores = jnp.einsum(
        "rhgd,rhld->rhgl", query_head_count, key_cache, preferred_element_type=jnp.float32
    ) * (1.0 / math.sqrt(head_dim))
    valid_mask = (jnp.arange(cache_len, dtype=jnp.int32)[None, :] < cache_lengths[:, None])[
        :, None, None, :
    ]
    scores = jnp.where(valid_mask, scores, -jnp.inf)
    largest = jnp.max(scores, axis=-1, keepdims=True)
    exponent = jnp.exp(scores - largest)
    attn_probs = (exponent / jnp.sum(exponent, axis=-1, keepdims=True)).astype(jnp.bfloat16)
    attn_out = jnp.einsum(
        "rhgl,rhld->rhgd", attn_probs, cached_value_rows, preferred_element_type=jnp.float32
    ).astype(jnp.bfloat16)
    attn_out = attn_out.reshape(rows_dev, kv_local * groups * head_dim)

    w_other = lax.ppermute(out_weight, "c", [(i, (i + 1) % n_c) for i in range(n_c)])
    w_lo = jnp.where(c_rank == 0, out_weight, w_other)
    w_hi = jnp.where(c_rank == 0, w_other, out_weight)
    w_pair = jnp.concatenate([w_lo, w_hi], axis=1)
    sent = jnp.broadcast_to(attn_out[None], (n_xz,) + attn_out.shape)
    mine = lax.all_to_all(sent, ("x", "z"), 0, 0, tiled=True)
    partial_value = jnp.einsum(
        "ird,dc->irc", mine, w_pair, preferred_element_type=jnp.float32
    ).astype(jnp.bfloat16)

    pair_cols = n_c * col_block
    sent = jnp.broadcast_to(partial_value[:, None], (n_xz, tp_count, rows_dev, pair_cols))
    got = lax.all_to_all(
        sent.reshape(n_xz * tp_count, rows_dev, pair_cols), ("x", "z", "tensor"), 0, 0, tiled=True
    )
    projected = got.reshape(n_xz, tp_count, rows_dev, pair_cols).astype(jnp.float32).sum(1)
    projected = projected.transpose(1, 0, 2).reshape(rows_dev, model_width).astype(jnp.bfloat16)
    residual, normed = residual_norm(hidden_in, projected)

    exp_dev = w_gate.shape[0]
    n_exp = n_all * exp_dev
    matches = expert_ids[:, :, None] == jnp.arange(n_exp, dtype=jnp.int32)[None, None, :]
    assigned = jnp.sum(matches.astype(jnp.int32), axis=1)
    slot_rank = jnp.cumsum(assigned, axis=0) - assigned
    slot_hit = (slot_rank[:, :, None] == jnp.arange(CAP, dtype=jnp.int32)[None, None, :]) & (
        assigned[:, :, None] > 0
    )
    route_weights = route_probs / jnp.sum(route_probs, axis=-1, keepdims=True)
    all_weight = jnp.sum(jnp.where(matches, route_weights[:, :, None], 0.0), axis=1)

    hit_col = slot_hit.reshape(rows_dev, dp_count, tp_count, exp_dev, CAP)
    hit_col = lax.dynamic_index_in_dim(hit_col, tp_rank, axis=2, keepdims=False)
    outgoing = jnp.einsum(
        "rmjc,rd->mjcd", hit_col.astype(jnp.bfloat16), normed, preferred_element_type=jnp.float32
    ).astype(jnp.bfloat16)
    arrived_slots = lax.all_to_all(outgoing, DP, 0, 0, tiled=True)
    gate_proj = jnp.einsum(
        "sjcd,jdf->sjcf", arrived_slots, w_gate, preferred_element_type=jnp.float32
    )
    up_proj = jnp.einsum("sjcd,jdf->sjcf", arrived_slots, w_up, preferred_element_type=jnp.float32)
    activated = (jax.nn.silu(gate_proj) * up_proj).astype(jnp.bfloat16)
    expert_out = jnp.einsum(
        "sjcf,jfd->sjcd", activated, w_down, preferred_element_type=jnp.float32
    ).astype(jnp.bfloat16)

    width_share = model_width // tp_count
    back = expert_out.reshape(dp_count, exp_dev, CAP, tp_count, width_share)
    back = back.transpose(0, 3, 1, 2, 4).reshape(n_all, exp_dev * CAP, width_share)
    results = lax.all_to_all(back, ALL, 0, 0, tiled=True)
    combine_table = jnp.where(slot_hit, all_weight[:, :, None], 0.0)
    mixture = jnp.einsum(
        "rmc,mcd->rd",
        combine_table,
        results.reshape(n_exp, CAP, width_share).astype(jnp.float32),
        precision=lax.Precision.HIGHEST,
    )
    residual_own = lax.dynamic_slice_in_dim(residual, tp_rank * width_share, width_share, 1)
    return (residual_own.astype(jnp.float32) + mixture).astype(jnp.bfloat16)


def split_mesh(mesh):
    devices = np.asarray(mesh.devices)
    n_dp, n_t = devices.shape
    n_c = 2
    try:
        xs = sorted({d.coords[0] for d in devices.flat})
        n_x = len(xs)
    except Exception:
        n_x = 4
    n_z = n_dp // (n_x * n_c)
    return Mesh(devices.reshape(n_x, n_z, n_c, n_t), ALL)


def solution(mesh):
    fine = split_mesh(mesh)
    placed = (
        P(DP, None),
        P(DP, "tensor"),
        P(DP, "tensor", None, None),
        P(DP, "tensor", None, None),
        P(DP),
        P("tensor", DP),
        P(DP, None),
        P(DP, None),
        P(ALL, None, None),
        P(ALL, None, None),
        P(ALL, None, None),
    )
    return jax.shard_map(
        local, mesh=fine, in_specs=placed, out_specs=P(DP, "tensor"), check_vma=False
    )
```

```python
import math

import jax
import jax.numpy as jnp
import numpy as np
from jax import lax
from jax.experimental import pallas as pl
from jax.experimental.pallas import tpu as pltpu
from jax.sharding import Mesh, PartitionSpec as P

CAP = 2
DP = ("x", "z", "c")
ALL = ("x", "z", "c", "tensor")


def residual_norm(hidden_rows, projected):
    residual = (hidden_rows.astype(jnp.float32) + projected.astype(jnp.float32)).astype(
        jnp.bfloat16
    )
    resid_f = residual.astype(jnp.float32)
    normed = (
        resid_f * lax.rsqrt(jnp.mean(resid_f * resid_f, axis=-1, keepdims=True) + 1e-06)
    ).astype(jnp.bfloat16)
    return (residual, normed)


def ffn_kernel(x_ref, wg_ref, wu_ref, wd_ref, o_ref, acc_ref):
    step = pl.program_id(0)

    @pl.when(step == 0)
    def _():
        acc_ref[...] = jnp.zeros_like(acc_ref)

    wg = wg_ref[...]
    wu = wu_ref[...]
    wd = wd_ref[...]
    for c in range(x_ref.shape[1]):
        x = x_ref[:, c, :]
        gate = jnp.dot(x, wg, preferred_element_type=jnp.float32)
        up = jnp.dot(x, wu, preferred_element_type=jnp.float32)
        activated = (gate / (1.0 + jnp.exp(-gate)) * up).astype(jnp.bfloat16)
        acc_ref[:, c, :] += jnp.dot(activated, wd, preferred_element_type=jnp.float32)

    @pl.when(step == pl.num_programs(0) - 1)
    def _():
        o_ref[...] = acc_ref[...].astype(o_ref.dtype)


def expert_ffn(x, wg, wu, wd, chunk=256):
    sources, slots, width = x.shape
    ff = wg.shape[1]
    return pl.pallas_call(
        ffn_kernel,
        grid=(ff // chunk,),
        in_specs=[
            pl.BlockSpec((sources, slots, width), lambda f: (0, 0, 0)),
            pl.BlockSpec((width, chunk), lambda f: (0, f)),
            pl.BlockSpec((width, chunk), lambda f: (0, f)),
            pl.BlockSpec((chunk, width), lambda f: (f, 0)),
        ],
        out_specs=pl.BlockSpec((sources, slots, width), lambda f: (0, 0, 0)),
        out_shape=jax.ShapeDtypeStruct((sources, slots, width), jnp.bfloat16),
        scratch_shapes=[pltpu.VMEM((sources, slots, width), jnp.float32)],
        compiler_params=pltpu.CompilerParams(vmem_limit_bytes=60 * 1024 * 1024),
        cost_estimate=pl.CostEstimate(
            flops=6 * sources * slots * width * ff,
            transcendentals=sources * slots * ff,
            bytes_accessed=2 * (3 * width * ff + 2 * sources * slots * width),
        ),
    )(x, wg, wu, wd)


def local(
    hidden_in,
    queries,
    key_cache,
    cached_value_rows,
    cache_lengths,
    out_weight,
    expert_ids,
    route_probs,
    w_gate,
    w_up,
    w_down,
):
    n_xz = lax.axis_size("x") * lax.axis_size("z")
    n_c = lax.axis_size("c")
    dp_count = n_xz * n_c
    tp_count = lax.axis_size("tensor")
    tp_rank = lax.axis_index("tensor")
    c_rank = lax.axis_index("c")
    rows_dev, kv_local, cache_len, head_dim = key_cache.shape
    groups = queries.shape[1] // (kv_local * head_dim)
    model_width = hidden_in.shape[1]
    col_block = model_width // dp_count
    n_all = dp_count * tp_count

    query_head_count = queries.reshape(rows_dev, kv_local, groups, head_dim)
    scores = jnp.einsum(
        "rhgd,rhld->rhgl", query_head_count, key_cache, preferred_element_type=jnp.float32
    ) * (1.0 / math.sqrt(head_dim))
    valid_mask = (jnp.arange(cache_len, dtype=jnp.int32)[None, :] < cache_lengths[:, None])[
        :, None, None, :
    ]
    scores = jnp.where(valid_mask, scores, -jnp.inf)
    largest = jnp.max(scores, axis=-1, keepdims=True)
    exponent = jnp.exp(scores - largest)
    attn_probs = (exponent / jnp.sum(exponent, axis=-1, keepdims=True)).astype(jnp.bfloat16)
    attn_out = jnp.einsum(
        "rhgl,rhld->rhgd", attn_probs, cached_value_rows, preferred_element_type=jnp.float32
    ).astype(jnp.bfloat16)
    attn_out = attn_out.reshape(rows_dev, kv_local * groups * head_dim)

    w_other = lax.ppermute(out_weight, "c", [(i, (i + 1) % n_c) for i in range(n_c)])
    w_lo = jnp.where(c_rank == 0, out_weight, w_other)
    w_hi = jnp.where(c_rank == 0, w_other, out_weight)
    w_pair = jnp.concatenate([w_lo, w_hi], axis=1)
    sent = jnp.broadcast_to(attn_out[None], (n_xz,) + attn_out.shape)
    mine = lax.all_to_all(sent, ("x", "z"), 0, 0, tiled=True)
    partial_value = jnp.einsum(
        "ird,dc->irc", mine, w_pair, preferred_element_type=jnp.float32
    ).astype(jnp.bfloat16)

    pair_cols = n_c * col_block
    sent = jnp.broadcast_to(partial_value[:, None], (n_xz, tp_count, rows_dev, pair_cols))
    got = lax.all_to_all(
        sent.reshape(n_xz * tp_count, rows_dev, pair_cols), ("x", "z", "tensor"), 0, 0, tiled=True
    )
    projected = got.reshape(n_xz, tp_count, rows_dev, pair_cols).astype(jnp.float32).sum(1)
    projected = projected.transpose(1, 0, 2).reshape(rows_dev, model_width).astype(jnp.bfloat16)
    residual, normed = residual_norm(hidden_in, projected)

    exp_dev = w_gate.shape[0]
    n_exp = n_all * exp_dev
    matches = expert_ids[:, :, None] == jnp.arange(n_exp, dtype=jnp.int32)[None, None, :]
    assigned = jnp.sum(matches.astype(jnp.int32), axis=1)
    slot_rank = jnp.cumsum(assigned, axis=0) - assigned
    slot_hit = (slot_rank[:, :, None] == jnp.arange(CAP, dtype=jnp.int32)[None, None, :]) & (
        assigned[:, :, None] > 0
    )
    route_weights = route_probs / jnp.sum(route_probs, axis=-1, keepdims=True)
    all_weight = jnp.sum(jnp.where(matches, route_weights[:, :, None], 0.0), axis=1)

    hit_col = slot_hit.reshape(rows_dev, dp_count, tp_count, exp_dev, CAP)
    hit_col = lax.dynamic_index_in_dim(hit_col, tp_rank, axis=2, keepdims=False)
    outgoing = jnp.einsum(
        "rmjc,rd->mjcd", hit_col.astype(jnp.bfloat16), normed, preferred_element_type=jnp.float32
    ).astype(jnp.bfloat16)
    arrived_slots = lax.all_to_all(outgoing, DP, 0, 0, tiled=True)
    assert exp_dev == 1
    expert_out = expert_ffn(
        arrived_slots.reshape(dp_count, CAP, model_width), w_gate[0], w_up[0], w_down[0]
    ).reshape(dp_count, exp_dev, CAP, model_width)

    width_share = model_width // tp_count
    back = expert_out.reshape(dp_count, exp_dev, CAP, tp_count, width_share)
    back = back.transpose(0, 3, 1, 2, 4).reshape(n_all, exp_dev * CAP, width_share)
    results = lax.all_to_all(back, ALL, 0, 0, tiled=True)
    combine_table = jnp.where(slot_hit, all_weight[:, :, None], 0.0)
    mixture = jnp.einsum(
        "rmc,mcd->rd",
        combine_table,
        results.reshape(n_exp, CAP, width_share).astype(jnp.float32),
        precision=lax.Precision.HIGHEST,
    )
    residual_own = lax.dynamic_slice_in_dim(residual, tp_rank * width_share, width_share, 1)
    return (residual_own.astype(jnp.float32) + mixture).astype(jnp.bfloat16)


def split_mesh(mesh):
    devices = np.asarray(mesh.devices)
    n_dp, n_t = devices.shape
    n_c = 2
    try:
        xs = sorted({d.coords[0] for d in devices.flat})
        n_x = len(xs)
    except Exception:
        n_x = 4
    n_z = n_dp // (n_x * n_c)
    return Mesh(devices.reshape(n_x, n_z, n_c, n_t), ALL)


def solution(mesh):
    fine = split_mesh(mesh)
    placed = (
        P(DP, None),
        P(DP, "tensor"),
        P(DP, "tensor", None, None),
        P(DP, "tensor", None, None),
        P(DP),
        P("tensor", DP),
        P(DP, None),
        P(DP, None),
        P(ALL, None, None),
        P(ALL, None, None),
        P(ALL, None, None),
    )
    return jax.shard_map(
        local, mesh=fine, in_specs=placed, out_specs=P(DP, "tensor"), check_vma=False
    )
```

```python
import math

import jax
import jax.numpy as jnp
import numpy as np
from jax import lax
from jax.experimental import pallas as pl
from jax.experimental.pallas import tpu as pltpu
from jax.sharding import Mesh, PartitionSpec as P

CAP = 2
DP = ("x", "z", "c")
ALL = ("x", "z", "c", "tensor")


def residual_norm(hidden_rows, projected):
    residual = (hidden_rows.astype(jnp.float32) + projected.astype(jnp.float32)).astype(
        jnp.bfloat16
    )
    resid_f = residual.astype(jnp.float32)
    normed = (
        resid_f * lax.rsqrt(jnp.mean(resid_f * resid_f, axis=-1, keepdims=True) + 1e-06)
    ).astype(jnp.bfloat16)
    return (residual, normed)


def ffn_kernel(x_ref, wg_ref, wu_ref, wd_ref, o_ref, acc_ref, out_ref):
    step = pl.program_id(0)
    sources, slots, _ = x_ref.shape
    parts = o_ref.shape[1]
    share = o_ref.shape[3]

    @pl.when(step == 0)
    def _():
        acc_ref[...] = jnp.zeros_like(acc_ref)

    x = jnp.concatenate([x_ref[:, c, :] for c in range(slots)], axis=0)
    gate = jnp.dot(x, wg_ref[...], preferred_element_type=jnp.float32)
    up = jnp.dot(x, wu_ref[...], preferred_element_type=jnp.float32)
    activated = (gate / (1.0 + jnp.exp(-gate)) * up).astype(jnp.bfloat16)
    acc_ref[...] += jnp.dot(activated, wd_ref[...], preferred_element_type=jnp.float32)

    @pl.when(step == pl.num_programs(0) - 1)
    def _():
        for t in range(parts):
            for c in range(slots):
                out_ref[:, t, c, :] = acc_ref[c * sources : (c + 1) * sources, t * share : (t + 1) * share]
        o_ref[...] = out_ref[...].astype(o_ref.dtype)


def expert_ffn(x, wg, wu, wd, parts, chunk=256):
    sources, slots, width = x.shape
    ff = wg.shape[1]
    share = width // parts
    return pl.pallas_call(
        ffn_kernel,
        grid=(ff // chunk,),
        in_specs=[
            pl.BlockSpec((sources, slots, width), lambda f: (0, 0, 0)),
            pl.BlockSpec((width, chunk), lambda f: (0, f)),
            pl.BlockSpec((width, chunk), lambda f: (0, f)),
            pl.BlockSpec((chunk, width), lambda f: (f, 0)),
        ],
        out_specs=pl.BlockSpec((sources, parts, slots, share), lambda f: (0, 0, 0, 0)),
        out_shape=jax.ShapeDtypeStruct((sources, parts, slots, share), jnp.bfloat16),
        scratch_shapes=[
            pltpu.VMEM((slots * sources, width), jnp.float32),
            pltpu.VMEM((sources, parts, slots, share), jnp.float32),
        ],
        compiler_params=pltpu.CompilerParams(vmem_limit_bytes=60 * 1024 * 1024),
        cost_estimate=pl.CostEstimate(
            flops=6 * sources * slots * width * ff,
            transcendentals=sources * slots * ff,
            bytes_accessed=2 * (3 * width * ff + 2 * sources * slots * width),
        ),
    )(x, wg, wu, wd)


def local(
    hidden_in,
    queries,
    key_cache,
    cached_value_rows,
    cache_lengths,
    out_weight,
    expert_ids,
    route_probs,
    w_gate,
    w_up,
    w_down,
):
    n_xz = lax.axis_size("x") * lax.axis_size("z")
    n_c = lax.axis_size("c")
    dp_count = n_xz * n_c
    tp_count = lax.axis_size("tensor")
    tp_rank = lax.axis_index("tensor")
    c_rank = lax.axis_index("c")
    rows_dev, kv_local, cache_len, head_dim = key_cache.shape
    groups = queries.shape[1] // (kv_local * head_dim)
    model_width = hidden_in.shape[1]
    col_block = model_width // dp_count
    n_all = dp_count * tp_count

    query_head_count = queries.reshape(rows_dev, kv_local, groups, head_dim)
    scores = jnp.einsum(
        "rhgd,rhld->rhgl", query_head_count, key_cache, preferred_element_type=jnp.float32
    ) * (1.0 / math.sqrt(head_dim))
    valid_mask = (jnp.arange(cache_len, dtype=jnp.int32)[None, :] < cache_lengths[:, None])[
        :, None, None, :
    ]
    scores = jnp.where(valid_mask, scores, -jnp.inf)
    largest = jnp.max(scores, axis=-1, keepdims=True)
    exponent = jnp.exp(scores - largest)
    attn_probs = (exponent / jnp.sum(exponent, axis=-1, keepdims=True)).astype(jnp.bfloat16)
    attn_out = jnp.einsum(
        "rhgl,rhld->rhgd", attn_probs, cached_value_rows, preferred_element_type=jnp.float32
    ).astype(jnp.bfloat16)
    attn_out = attn_out.reshape(rows_dev, kv_local * groups * head_dim)

    w_other = lax.ppermute(out_weight, "c", [(i, (i + 1) % n_c) for i in range(n_c)])
    w_lo = jnp.where(c_rank == 0, out_weight, w_other)
    w_hi = jnp.where(c_rank == 0, w_other, out_weight)
    w_pair = jnp.concatenate([w_lo, w_hi], axis=1)
    sent = jnp.broadcast_to(attn_out[None], (n_xz,) + attn_out.shape)
    mine = lax.all_to_all(sent, ("x", "z"), 0, 0, tiled=True)
    partial_value = jnp.einsum(
        "ird,dc->irc", mine, w_pair, preferred_element_type=jnp.float32
    ).astype(jnp.bfloat16)

    pair_cols = n_c * col_block
    sent = jnp.broadcast_to(partial_value[:, None], (n_xz, tp_count, rows_dev, pair_cols))
    got = lax.all_to_all(
        sent.reshape(n_xz * tp_count, rows_dev, pair_cols), ("x", "z", "tensor"), 0, 0, tiled=True
    )
    projected = got.reshape(n_xz, tp_count, rows_dev, pair_cols).astype(jnp.float32).sum(1)
    projected = projected.transpose(1, 0, 2).reshape(rows_dev, model_width).astype(jnp.bfloat16)
    residual, normed = residual_norm(hidden_in, projected)

    exp_dev = w_gate.shape[0]
    n_exp = n_all * exp_dev
    matches = expert_ids[:, :, None] == jnp.arange(n_exp, dtype=jnp.int32)[None, None, :]
    assigned = jnp.sum(matches.astype(jnp.int32), axis=1)
    slot_rank = jnp.cumsum(assigned, axis=0) - assigned
    slot_hit = (slot_rank[:, :, None] == jnp.arange(CAP, dtype=jnp.int32)[None, None, :]) & (
        assigned[:, :, None] > 0
    )
    route_weights = route_probs / jnp.sum(route_probs, axis=-1, keepdims=True)
    all_weight = jnp.sum(jnp.where(matches, route_weights[:, :, None], 0.0), axis=1)

    hit_col = slot_hit.reshape(rows_dev, dp_count, tp_count, exp_dev, CAP)
    hit_col = lax.dynamic_index_in_dim(hit_col, tp_rank, axis=2, keepdims=False)
    outgoing = jnp.einsum(
        "rmjc,rd->mjcd", hit_col.astype(jnp.bfloat16), normed, preferred_element_type=jnp.float32
    ).astype(jnp.bfloat16)
    arrived_slots = lax.all_to_all(outgoing, DP, 0, 0, tiled=True)
    assert exp_dev == 1
    width_share = model_width // tp_count
    back = expert_ffn(
        arrived_slots.reshape(dp_count, CAP, model_width), w_gate[0], w_up[0], w_down[0], tp_count
    ).reshape(n_all, exp_dev * CAP, width_share)

    results = lax.all_to_all(back, ALL, 0, 0, tiled=True)
    combine_table = jnp.where(slot_hit, all_weight[:, :, None], 0.0)
    mixture = jnp.einsum(
        "rmc,mcd->rd",
        combine_table,
        results.reshape(n_exp, CAP, width_share).astype(jnp.float32),
        precision=lax.Precision.HIGHEST,
    )
    residual_own = lax.dynamic_slice_in_dim(residual, tp_rank * width_share, width_share, 1)
    return (residual_own.astype(jnp.float32) + mixture).astype(jnp.bfloat16)


def split_mesh(mesh):
    devices = np.asarray(mesh.devices)
    n_dp, n_t = devices.shape
    n_c = 2
    try:
        xs = sorted({d.coords[0] for d in devices.flat})
        n_x = len(xs)
    except Exception:
        n_x = 4
    n_z = n_dp // (n_x * n_c)
    return Mesh(devices.reshape(n_x, n_z, n_c, n_t), ALL)


def solution(mesh):
    fine = split_mesh(mesh)
    placed = (
        P(DP, None),
        P(DP, "tensor"),
        P(DP, "tensor", None, None),
        P(DP, "tensor", None, None),
        P(DP),
        P("tensor", DP),
        P(DP, None),
        P(DP, None),
        P(ALL, None, None),
        P(ALL, None, None),
        P(ALL, None, None),
    )
    return jax.shard_map(
        local, mesh=fine, in_specs=placed, out_specs=P(DP, "tensor"), check_vma=False
    )
```

```python
import math

import jax
import jax.numpy as jnp
import numpy as np
from jax import lax
from jax.experimental import pallas as pl
from jax.experimental.pallas import tpu as pltpu
from jax.sharding import Mesh, PartitionSpec as P

CAP = 2
DP = ("x", "z", "c")
ALL = ("x", "z", "c", "tensor")


def residual_norm(hidden_rows, projected):
    residual = (hidden_rows.astype(jnp.float32) + projected.astype(jnp.float32)).astype(
        jnp.bfloat16
    )
    resid_f = residual.astype(jnp.float32)
    normed = (
        resid_f * lax.rsqrt(jnp.mean(resid_f * resid_f, axis=-1, keepdims=True) + 1e-06)
    ).astype(jnp.bfloat16)
    return (residual, normed)


def ffn_kernel(x_ref, *refs):
    *w_refs, o_ref, acc_ref, out_ref = refs
    step = pl.program_id(0)
    sources, slots, _ = x_ref.shape
    parts = o_ref.shape[1]
    share = o_ref.shape[3]

    @pl.when(step == 0)
    def _():
        acc_ref[...] = jnp.zeros_like(acc_ref)

    x = jnp.concatenate([x_ref[:, c, :] for c in range(slots)], axis=0)
    for wg_ref, wu_ref, wd_ref in zip(w_refs[0::3], w_refs[1::3], w_refs[2::3]):
        gate = jnp.dot(x, wg_ref[...], preferred_element_type=jnp.float32)
        up = jnp.dot(x, wu_ref[...], preferred_element_type=jnp.float32)
        activated = (gate / (1.0 + jnp.exp(-gate)) * up).astype(jnp.bfloat16)
        acc_ref[...] += jnp.dot(activated, wd_ref[...], preferred_element_type=jnp.float32)

    @pl.when(step == pl.num_programs(0) - 1)
    def _():
        for t in range(parts):
            for c in range(slots):
                out_ref[:, t, c, :] = acc_ref[c * sources : (c + 1) * sources, t * share : (t + 1) * share]
        o_ref[...] = out_ref[...].astype(o_ref.dtype)


def expert_ffn(x, wg, wu, wd, parts, chunk=256, split=2):
    sources, slots, width = x.shape
    ff = wg.shape[1]
    share = width // parts
    return pl.pallas_call(
        ffn_kernel,
        grid=(ff // chunk,),
        in_specs=[pl.BlockSpec((sources, slots, width), lambda f: (0, 0, 0))]
        + [
            spec
            for h in range(split)
            for spec in (
                pl.BlockSpec((width, chunk // split), lambda f, h=h: (0, f * split + h)),
                pl.BlockSpec((width, chunk // split), lambda f, h=h: (0, f * split + h)),
                pl.BlockSpec((chunk // split, width), lambda f, h=h: (f * split + h, 0)),
            )
        ],
        out_specs=pl.BlockSpec((sources, parts, slots, share), lambda f: (0, 0, 0, 0)),
        out_shape=jax.ShapeDtypeStruct((sources, parts, slots, share), jnp.bfloat16),
        scratch_shapes=[
            pltpu.VMEM((slots * sources, width), jnp.float32),
            pltpu.VMEM((sources, parts, slots, share), jnp.float32),
        ],
        compiler_params=pltpu.CompilerParams(vmem_limit_bytes=60 * 1024 * 1024),
        cost_estimate=pl.CostEstimate(
            flops=6 * sources * slots * width * ff,
            transcendentals=sources * slots * ff,
            bytes_accessed=2 * (3 * width * ff + 2 * sources * slots * width),
        ),
    )(x, *([wg, wu, wd] * split))


def local(
    hidden_in,
    queries,
    key_cache,
    cached_value_rows,
    cache_lengths,
    out_weight,
    expert_ids,
    route_probs,
    w_gate,
    w_up,
    w_down,
):
    n_xz = lax.axis_size("x") * lax.axis_size("z")
    n_c = lax.axis_size("c")
    dp_count = n_xz * n_c
    tp_count = lax.axis_size("tensor")
    tp_rank = lax.axis_index("tensor")
    c_rank = lax.axis_index("c")
    rows_dev, kv_local, cache_len, head_dim = key_cache.shape
    groups = queries.shape[1] // (kv_local * head_dim)
    model_width = hidden_in.shape[1]
    col_block = model_width // dp_count
    n_all = dp_count * tp_count

    query_head_count = queries.reshape(rows_dev, kv_local, groups, head_dim)
    scores = jnp.einsum(
        "rhgd,rhld->rhgl", query_head_count, key_cache, preferred_element_type=jnp.float32
    ) * (1.0 / math.sqrt(head_dim))
    valid_mask = (jnp.arange(cache_len, dtype=jnp.int32)[None, :] < cache_lengths[:, None])[
        :, None, None, :
    ]
    scores = jnp.where(valid_mask, scores, -jnp.inf)
    largest = jnp.max(scores, axis=-1, keepdims=True)
    exponent = jnp.exp(scores - largest)
    attn_probs = (exponent / jnp.sum(exponent, axis=-1, keepdims=True)).astype(jnp.bfloat16)
    attn_out = jnp.einsum(
        "rhgl,rhld->rhgd", attn_probs, cached_value_rows, preferred_element_type=jnp.float32
    ).astype(jnp.bfloat16)
    attn_out = attn_out.reshape(rows_dev, kv_local * groups * head_dim)

    w_other = lax.ppermute(out_weight, "c", [(i, (i + 1) % n_c) for i in range(n_c)])
    w_lo = jnp.where(c_rank == 0, out_weight, w_other)
    w_hi = jnp.where(c_rank == 0, w_other, out_weight)
    w_pair = jnp.concatenate([w_lo, w_hi], axis=1)
    sent = jnp.broadcast_to(attn_out[None], (n_xz,) + attn_out.shape)
    mine = lax.all_to_all(sent, ("x", "z"), 0, 0, tiled=True)
    partial_value = jnp.einsum(
        "ird,dc->irc", mine, w_pair, preferred_element_type=jnp.float32
    ).astype(jnp.bfloat16)

    pair_cols = n_c * col_block
    sent = jnp.broadcast_to(partial_value[:, None], (n_xz, tp_count, rows_dev, pair_cols))
    got = lax.all_to_all(
        sent.reshape(n_xz * tp_count, rows_dev, pair_cols), ("x", "z", "tensor"), 0, 0, tiled=True
    )
    projected = got.reshape(n_xz, tp_count, rows_dev, pair_cols).astype(jnp.float32).sum(1)
    projected = projected.transpose(1, 0, 2).reshape(rows_dev, model_width).astype(jnp.bfloat16)
    residual, normed = residual_norm(hidden_in, projected)

    exp_dev = w_gate.shape[0]
    n_exp = n_all * exp_dev
    matches = expert_ids[:, :, None] == jnp.arange(n_exp, dtype=jnp.int32)[None, None, :]
    assigned = jnp.sum(matches.astype(jnp.int32), axis=1)
    slot_rank = jnp.cumsum(assigned, axis=0) - assigned
    slot_hit = (slot_rank[:, :, None] == jnp.arange(CAP, dtype=jnp.int32)[None, None, :]) & (
        assigned[:, :, None] > 0
    )
    route_weights = route_probs / jnp.sum(route_probs, axis=-1, keepdims=True)
    all_weight = jnp.sum(jnp.where(matches, route_weights[:, :, None], 0.0), axis=1)

    hit_col = slot_hit.reshape(rows_dev, dp_count, tp_count, exp_dev, CAP)
    hit_col = lax.dynamic_index_in_dim(hit_col, tp_rank, axis=2, keepdims=False)
    outgoing = jnp.einsum(
        "rmjc,rd->mjcd", hit_col.astype(jnp.bfloat16), normed, preferred_element_type=jnp.float32
    ).astype(jnp.bfloat16)
    arrived_slots = lax.all_to_all(outgoing, DP, 0, 0, tiled=True)
    assert exp_dev == 1
    width_share = model_width // tp_count
    back = expert_ffn(
        arrived_slots.reshape(dp_count, CAP, model_width), w_gate[0], w_up[0], w_down[0], tp_count
    ).reshape(n_all, exp_dev * CAP, width_share)

    results = lax.all_to_all(back, ALL, 0, 0, tiled=True)
    combine_table = jnp.where(slot_hit, all_weight[:, :, None], 0.0)
    mixture = jnp.einsum(
        "rmc,mcd->rd",
        combine_table,
        results.reshape(n_exp, CAP, width_share).astype(jnp.float32),
        precision=lax.Precision.HIGHEST,
    )
    residual_own = lax.dynamic_slice_in_dim(residual, tp_rank * width_share, width_share, 1)
    return (residual_own.astype(jnp.float32) + mixture).astype(jnp.bfloat16)


def split_mesh(mesh):
    devices = np.asarray(mesh.devices)
    n_dp, n_t = devices.shape
    n_c = 2
    try:
        xs = sorted({d.coords[0] for d in devices.flat})
        n_x = len(xs)
    except Exception:
        n_x = 4
    n_z = n_dp // (n_x * n_c)
    return Mesh(devices.reshape(n_x, n_z, n_c, n_t), ALL)


def solution(mesh):
    fine = split_mesh(mesh)
    placed = (
        P(DP, None),
        P(DP, "tensor"),
        P(DP, "tensor", None, None),
        P(DP, "tensor", None, None),
        P(DP),
        P("tensor", DP),
        P(DP, None),
        P(DP, None),
        P(ALL, None, None),
        P(ALL, None, None),
        P(ALL, None, None),
    )
    return jax.shard_map(
        local, mesh=fine, in_specs=placed, out_specs=P(DP, "tensor"), check_vma=False
    )
```

```python
import math

import jax
import jax.numpy as jnp
import numpy as np
from jax import lax
from jax.experimental import pallas as pl
from jax.experimental.pallas import tpu as pltpu
from jax.sharding import Mesh, PartitionSpec as P

CAP = 2
DP = ("x", "z", "c")
ALL = ("x", "z", "c", "tensor")


def residual_norm(hidden_rows, projected):
    residual = (hidden_rows.astype(jnp.float32) + projected.astype(jnp.float32)).astype(
        jnp.bfloat16
    )
    resid_f = residual.astype(jnp.float32)
    normed = (
        resid_f * lax.rsqrt(jnp.mean(resid_f * resid_f, axis=-1, keepdims=True) + 1e-06)
    ).astype(jnp.bfloat16)
    return (residual, normed)


def ffn_kernel(x_ref, wg_ref, wu_ref, wd_ref, o_ref, acc_ref, out_ref):
    step = pl.program_id(0)
    sources, slots, _ = x_ref.shape
    parts = o_ref.shape[1]
    share = o_ref.shape[3]

    @pl.when(step == 0)
    def _():
        acc_ref[...] = jnp.zeros_like(acc_ref)

    x = jnp.concatenate([x_ref[:, c, :] for c in range(slots)], axis=0)
    gate = jnp.dot(x, wg_ref[...], preferred_element_type=jnp.float32)
    up = jnp.dot(x, wu_ref[...], preferred_element_type=jnp.float32)
    activated = (gate / (1.0 + jnp.exp(-gate)) * up).astype(jnp.bfloat16)
    acc_ref[...] += jnp.dot(activated, wd_ref[...], preferred_element_type=jnp.float32)

    @pl.when(step == pl.num_programs(0) - 1)
    def _():
        for t in range(parts):
            for c in range(slots):
                out_ref[:, t, c, :] = acc_ref[c * sources : (c + 1) * sources, t * share : (t + 1) * share]
        o_ref[...] = out_ref[...].astype(o_ref.dtype)


def expert_ffn(x, wg, wu, wd, parts, chunk=384):
    sources, slots, width = x.shape
    ff = wg.shape[1]
    share = width // parts
    return pl.pallas_call(
        ffn_kernel,
        grid=(ff // chunk,),
        in_specs=[
            pl.BlockSpec((sources, slots, width), lambda f: (0, 0, 0)),
            pl.BlockSpec((width, chunk), lambda f: (0, f)),
            pl.BlockSpec((width, chunk), lambda f: (0, f)),
            pl.BlockSpec((chunk, width), lambda f: (f, 0)),
        ],
        out_specs=pl.BlockSpec((sources, parts, slots, share), lambda f: (0, 0, 0, 0)),
        out_shape=jax.ShapeDtypeStruct((sources, parts, slots, share), jnp.bfloat16),
        scratch_shapes=[
            pltpu.VMEM((slots * sources, width), jnp.float32),
            pltpu.VMEM((sources, parts, slots, share), jnp.float32),
        ],
        compiler_params=pltpu.CompilerParams(vmem_limit_bytes=60 * 1024 * 1024),
        cost_estimate=pl.CostEstimate(
            flops=6 * sources * slots * width * ff,
            transcendentals=sources * slots * ff,
            bytes_accessed=2 * (3 * width * ff + 2 * sources * slots * width),
        ),
    )(x, wg, wu, wd)


def local(
    hidden_in,
    queries,
    key_cache,
    cached_value_rows,
    cache_lengths,
    out_weight,
    expert_ids,
    route_probs,
    w_gate,
    w_up,
    w_down,
):
    n_xz = lax.axis_size("x") * lax.axis_size("z")
    n_c = lax.axis_size("c")
    dp_count = n_xz * n_c
    tp_count = lax.axis_size("tensor")
    tp_rank = lax.axis_index("tensor")
    c_rank = lax.axis_index("c")
    rows_dev, kv_local, cache_len, head_dim = key_cache.shape
    groups = queries.shape[1] // (kv_local * head_dim)
    model_width = hidden_in.shape[1]
    col_block = model_width // dp_count
    n_all = dp_count * tp_count

    query_head_count = queries.reshape(rows_dev, kv_local, groups, head_dim)
    scores = jnp.einsum(
        "rhgd,rhld->rhgl", query_head_count, key_cache, preferred_element_type=jnp.float32
    ) * (1.0 / math.sqrt(head_dim))
    valid_mask = (jnp.arange(cache_len, dtype=jnp.int32)[None, :] < cache_lengths[:, None])[
        :, None, None, :
    ]
    scores = jnp.where(valid_mask, scores, -jnp.inf)
    largest = jnp.max(scores, axis=-1, keepdims=True)
    exponent = jnp.exp(scores - largest)
    attn_probs = (exponent / jnp.sum(exponent, axis=-1, keepdims=True)).astype(jnp.bfloat16)
    attn_out = jnp.einsum(
        "rhgl,rhld->rhgd", attn_probs, cached_value_rows, preferred_element_type=jnp.float32
    ).astype(jnp.bfloat16)
    attn_out = attn_out.reshape(rows_dev, kv_local * groups * head_dim)

    w_other = lax.ppermute(out_weight, "c", [(i, (i + 1) % n_c) for i in range(n_c)])
    w_lo = jnp.where(c_rank == 0, out_weight, w_other)
    w_hi = jnp.where(c_rank == 0, w_other, out_weight)
    w_pair = jnp.concatenate([w_lo, w_hi], axis=1)
    sent = jnp.broadcast_to(attn_out[None], (n_xz,) + attn_out.shape)
    mine = lax.all_to_all(sent, ("x", "z"), 0, 0, tiled=True)
    partial_value = jnp.einsum(
        "ird,dc->irc", mine, w_pair, preferred_element_type=jnp.float32
    ).astype(jnp.bfloat16)

    pair_cols = n_c * col_block
    sent = jnp.broadcast_to(partial_value[:, None], (n_xz, tp_count, rows_dev, pair_cols))
    got = lax.all_to_all(
        sent.reshape(n_xz * tp_count, rows_dev, pair_cols), ("x", "z", "tensor"), 0, 0, tiled=True
    )
    projected = got.reshape(n_xz, tp_count, rows_dev, pair_cols).astype(jnp.float32).sum(1)
    projected = projected.transpose(1, 0, 2).reshape(rows_dev, model_width).astype(jnp.bfloat16)
    residual, normed = residual_norm(hidden_in, projected)

    exp_dev = w_gate.shape[0]
    n_exp = n_all * exp_dev
    matches = expert_ids[:, :, None] == jnp.arange(n_exp, dtype=jnp.int32)[None, None, :]
    assigned = jnp.sum(matches.astype(jnp.int32), axis=1)
    slot_rank = jnp.cumsum(assigned, axis=0) - assigned
    slot_hit = (slot_rank[:, :, None] == jnp.arange(CAP, dtype=jnp.int32)[None, None, :]) & (
        assigned[:, :, None] > 0
    )
    route_weights = route_probs / jnp.sum(route_probs, axis=-1, keepdims=True)
    all_weight = jnp.sum(jnp.where(matches, route_weights[:, :, None], 0.0), axis=1)

    hit_col = slot_hit.reshape(rows_dev, dp_count, tp_count, exp_dev, CAP)
    hit_col = lax.dynamic_index_in_dim(hit_col, tp_rank, axis=2, keepdims=False)
    outgoing = jnp.einsum(
        "rmjc,rd->mjcd", hit_col.astype(jnp.bfloat16), normed, preferred_element_type=jnp.float32
    ).astype(jnp.bfloat16)
    arrived_slots = lax.all_to_all(outgoing, DP, 0, 0, tiled=True)
    assert exp_dev == 1
    width_share = model_width // tp_count
    back = expert_ffn(
        arrived_slots.reshape(dp_count, CAP, model_width), w_gate[0], w_up[0], w_down[0], tp_count
    ).reshape(n_all, exp_dev * CAP, width_share)

    results = lax.all_to_all(back, ALL, 0, 0, tiled=True)
    combine_table = jnp.where(slot_hit, all_weight[:, :, None], 0.0)
    mixture = jnp.einsum(
        "rmc,mcd->rd",
        combine_table,
        results.reshape(n_exp, CAP, width_share).astype(jnp.float32),
        precision=lax.Precision.HIGHEST,
    )
    residual_own = lax.dynamic_slice_in_dim(residual, tp_rank * width_share, width_share, 1)
    return (residual_own.astype(jnp.float32) + mixture).astype(jnp.bfloat16)


def split_mesh(mesh):
    devices = np.asarray(mesh.devices)
    n_dp, n_t = devices.shape
    n_c = 2
    try:
        xs = sorted({d.coords[0] for d in devices.flat})
        n_x = len(xs)
    except Exception:
        n_x = 4
    n_z = n_dp // (n_x * n_c)
    return Mesh(devices.reshape(n_x, n_z, n_c, n_t), ALL)


def solution(mesh):
    fine = split_mesh(mesh)
    placed = (
        P(DP, None),
        P(DP, "tensor"),
        P(DP, "tensor", None, None),
        P(DP, "tensor", None, None),
        P(DP),
        P("tensor", DP),
        P(DP, None),
        P(DP, None),
        P(ALL, None, None),
        P(ALL, None, None),
        P(ALL, None, None),
    )
    return jax.shard_map(
        local, mesh=fine, in_specs=placed, out_specs=P(DP, "tensor"), check_vma=False
    )
```

```python
import math

import jax
import jax.numpy as jnp
import numpy as np
from jax import lax
from jax.experimental import pallas as pl
from jax.experimental.pallas import tpu as pltpu
from jax.sharding import Mesh, PartitionSpec as P

CAP = 2
DP = ("x", "z", "c")
ALL = ("x", "z", "c", "tensor")


def residual_norm(hidden_rows, projected):
    residual = (hidden_rows.astype(jnp.float32) + projected.astype(jnp.float32)).astype(
        jnp.bfloat16
    )
    resid_f = residual.astype(jnp.float32)
    normed = (
        resid_f * lax.rsqrt(jnp.mean(resid_f * resid_f, axis=-1, keepdims=True) + 1e-06)
    ).astype(jnp.bfloat16)
    return (residual, normed)


def ffn_kernel(x_ref, wg_ref, wu_ref, wd_ref, o_ref, acc_ref, out_ref):
    step = pl.program_id(0)
    sources, slots, _ = x_ref.shape
    parts = o_ref.shape[1]
    share = o_ref.shape[3]

    @pl.when(step == 0)
    def _():
        acc_ref[...] = jnp.zeros_like(acc_ref)

    x = jnp.concatenate([x_ref[:, c, :] for c in range(slots)], axis=0)
    gate = jnp.dot(x, wg_ref[...], preferred_element_type=jnp.float32)
    up = jnp.dot(x, wu_ref[...], preferred_element_type=jnp.float32)
    activated = (gate / (1.0 + jnp.exp(-gate)) * up).astype(jnp.bfloat16)
    acc_ref[...] += jnp.dot(activated, wd_ref[...], preferred_element_type=jnp.float32)

    @pl.when(step == pl.num_programs(0) - 1)
    def _():
        for t in range(parts):
            for c in range(slots):
                out_ref[:, t, c, :] = acc_ref[c * sources : (c + 1) * sources, t * share : (t + 1) * share]
        o_ref[...] = out_ref[...].astype(o_ref.dtype)


def expert_ffn(x, wg, wu, wd, parts, chunk=256):
    sources, slots, width = x.shape
    ff = wg.shape[1]
    share = width // parts
    return pl.pallas_call(
        ffn_kernel,
        grid=(ff // chunk,),
        in_specs=[
            pl.BlockSpec((sources, slots, width), lambda f: (0, 0, 0)),
            pl.BlockSpec((width, chunk), lambda f: (0, f)),
            pl.BlockSpec((width, chunk), lambda f: (0, f)),
            pl.BlockSpec((chunk, width), lambda f: (f, 0)),
        ],
        out_specs=pl.BlockSpec((sources, parts, slots, share), lambda f: (0, 0, 0, 0)),
        out_shape=jax.ShapeDtypeStruct((sources, parts, slots, share), jnp.bfloat16),
        scratch_shapes=[
            pltpu.VMEM((slots * sources, width), jnp.float32),
            pltpu.VMEM((sources, parts, slots, share), jnp.float32),
        ],
        compiler_params=pltpu.CompilerParams(vmem_limit_bytes=60 * 1024 * 1024),
        cost_estimate=pl.CostEstimate(
            flops=6 * sources * slots * width * ff,
            transcendentals=sources * slots * ff,
            bytes_accessed=2 * (3 * width * ff + 2 * sources * slots * width),
        ),
    )(x, wg, wu, wd)


def local(
    hidden_in,
    queries,
    key_cache,
    cached_value_rows,
    cache_lengths,
    out_weight,
    expert_ids,
    route_probs,
    w_gate,
    w_up,
    w_down,
):
    n_xz = lax.axis_size("x") * lax.axis_size("z")
    n_c = lax.axis_size("c")
    dp_count = n_xz * n_c
    tp_count = lax.axis_size("tensor")
    tp_rank = lax.axis_index("tensor")
    c_rank = lax.axis_index("c")
    rows_dev, kv_local, cache_len, head_dim = key_cache.shape
    groups = queries.shape[1] // (kv_local * head_dim)
    model_width = hidden_in.shape[1]
    col_block = model_width // dp_count
    n_all = dp_count * tp_count

    query_head_count = queries.reshape(rows_dev, kv_local, groups, head_dim)
    scores = jnp.einsum(
        "rhgd,rhld->rhgl", query_head_count, key_cache, preferred_element_type=jnp.float32
    ) * (1.0 / math.sqrt(head_dim))
    valid_mask = (jnp.arange(cache_len, dtype=jnp.int32)[None, :] < cache_lengths[:, None])[
        :, None, None, :
    ]
    scores = jnp.where(valid_mask, scores, -jnp.inf)
    largest = jnp.max(scores, axis=-1, keepdims=True)
    exponent = jnp.exp(scores - largest)
    attn_probs = (exponent / jnp.sum(exponent, axis=-1, keepdims=True)).astype(jnp.bfloat16)
    attn_out = jnp.einsum(
        "rhgl,rhld->rhgd", attn_probs, cached_value_rows, preferred_element_type=jnp.float32
    ).astype(jnp.bfloat16)
    attn_out = attn_out.reshape(rows_dev, kv_local * groups * head_dim)

    w_other = lax.ppermute(out_weight, "c", [(i, (i + 1) % n_c) for i in range(n_c)])
    w_lo = jnp.where(c_rank == 0, out_weight, w_other)
    w_hi = jnp.where(c_rank == 0, w_other, out_weight)
    w_pair = jnp.concatenate([w_lo, w_hi], axis=1)
    sent = jnp.broadcast_to(attn_out[None], (n_xz,) + attn_out.shape)
    mine = lax.all_to_all(sent, ("x", "z"), 0, 0, tiled=True)
    partial_value = jnp.einsum(
        "ird,dc->irc", mine, w_pair, preferred_element_type=jnp.float32
    ).astype(jnp.bfloat16)

    pair_cols = n_c * col_block
    sent = jnp.broadcast_to(partial_value[:, None], (n_xz, tp_count, rows_dev, pair_cols))
    got = lax.all_to_all(
        sent.reshape(n_xz * tp_count, rows_dev, pair_cols), ("x", "z", "tensor"), 0, 0, tiled=True
    )
    projected = got.reshape(n_xz, tp_count, rows_dev, pair_cols).astype(jnp.float32).sum(1)
    projected = projected.transpose(1, 0, 2).reshape(rows_dev, model_width).astype(jnp.bfloat16)
    residual, normed = residual_norm(hidden_in, projected)

    exp_dev = w_gate.shape[0]
    n_exp = n_all * exp_dev
    matches = expert_ids[:, :, None] == jnp.arange(n_exp, dtype=jnp.int32)[None, None, :]
    assigned = jnp.sum(matches.astype(jnp.int32), axis=1)
    slot_rank = jnp.cumsum(assigned, axis=0) - assigned
    slot_hit = (slot_rank[:, :, None] == jnp.arange(CAP, dtype=jnp.int32)[None, None, :]) & (
        assigned[:, :, None] > 0
    )
    route_weights = route_probs / jnp.sum(route_probs, axis=-1, keepdims=True)
    all_weight = jnp.sum(jnp.where(matches, route_weights[:, :, None], 0.0), axis=1)

    hit_col = slot_hit.reshape(rows_dev, dp_count, tp_count, exp_dev, CAP)
    hit_col = lax.dynamic_index_in_dim(hit_col, tp_rank, axis=2, keepdims=False)
    outgoing = jnp.einsum(
        "rmjc,rd->mjcd", hit_col.astype(jnp.bfloat16), normed, preferred_element_type=jnp.float32
    ).astype(jnp.bfloat16)
    arrived_slots = lax.all_to_all(outgoing, DP, 0, 0, tiled=True)
    assert exp_dev == 1
    width_share = model_width // tp_count
    back = expert_ffn(
        arrived_slots.reshape(dp_count, CAP, model_width), w_gate[0], w_up[0], w_down[0], tp_count
    ).reshape(n_all, exp_dev * CAP, width_share)

    results = lax.all_to_all(back, ALL, 0, 0, tiled=True)
    combine_table = jnp.where(slot_hit, all_weight[:, :, None], 0.0)
    table_hi = combine_table.astype(jnp.bfloat16)
    table_lo = (combine_table - table_hi.astype(jnp.float32)).astype(jnp.bfloat16)
    arrived_out = results.reshape(n_exp, CAP, width_share)
    mixture = jnp.einsum(
        "rmc,mcd->rd", table_hi, arrived_out, preferred_element_type=jnp.float32
    ) + jnp.einsum("rmc,mcd->rd", table_lo, arrived_out, preferred_element_type=jnp.float32)
    residual_own = lax.dynamic_slice_in_dim(residual, tp_rank * width_share, width_share, 1)
    return (residual_own.astype(jnp.float32) + mixture).astype(jnp.bfloat16)


def split_mesh(mesh):
    devices = np.asarray(mesh.devices)
    n_dp, n_t = devices.shape
    n_c = 2
    try:
        xs = sorted({d.coords[0] for d in devices.flat})
        n_x = len(xs)
    except Exception:
        n_x = 4
    n_z = n_dp // (n_x * n_c)
    return Mesh(devices.reshape(n_x, n_z, n_c, n_t), ALL)


def solution(mesh):
    fine = split_mesh(mesh)
    placed = (
        P(DP, None),
        P(DP, "tensor"),
        P(DP, "tensor", None, None),
        P(DP, "tensor", None, None),
        P(DP),
        P("tensor", DP),
        P(DP, None),
        P(DP, None),
        P(ALL, None, None),
        P(ALL, None, None),
        P(ALL, None, None),
    )
    return jax.shard_map(
        local, mesh=fine, in_specs=placed, out_specs=P(DP, "tensor"), check_vma=False
    )
```

```python
import math

import jax
import jax.numpy as jnp
import numpy as np
from jax import lax
from jax.experimental import pallas as pl
from jax.experimental.pallas import tpu as pltpu
from jax.sharding import Mesh, PartitionSpec as P

CAP = 2
DP = ("x", "z", "c")
ALL = ("x", "z", "c", "tensor")


def residual_norm(hidden_rows, projected):
    residual = (hidden_rows.astype(jnp.float32) + projected.astype(jnp.float32)).astype(
        jnp.bfloat16
    )
    resid_f = residual.astype(jnp.float32)
    normed = (
        resid_f * lax.rsqrt(jnp.mean(resid_f * resid_f, axis=-1, keepdims=True) + 1e-06)
    ).astype(jnp.bfloat16)
    return (residual, normed)


def ffn_kernel(x_ref, wg_ref, wu_ref, wd_ref, o_ref, acc_ref):
    step = pl.program_id(0)
    sources, slots, _ = x_ref.shape
    parts = o_ref.shape[1]
    share = o_ref.shape[3]

    @pl.when(step == 0)
    def _():
        acc_ref[...] = jnp.zeros_like(acc_ref)

    x = jnp.concatenate([x_ref[:, c, :] for c in range(slots)], axis=0)
    gate = jnp.dot(x, wg_ref[...], preferred_element_type=jnp.float32)
    up = jnp.dot(x, wu_ref[...], preferred_element_type=jnp.float32)
    activated = (gate / (1.0 + jnp.exp(-gate)) * up).astype(jnp.bfloat16)
    acc_ref[...] += jnp.dot(activated, wd_ref[...], preferred_element_type=jnp.float32)

    @pl.when(step == pl.num_programs(0) - 1)
    def _():
        for t in range(parts):
            for c in range(slots):
                o_ref[:, t, c, :] = acc_ref[
                    c * sources : (c + 1) * sources, t * share : (t + 1) * share
                ].astype(o_ref.dtype)


def expert_ffn(x, wg, wu, wd, parts, chunk=256):
    sources, slots, width = x.shape
    ff = wg.shape[1]
    share = width // parts
    return pl.pallas_call(
        ffn_kernel,
        grid=(ff // chunk,),
        in_specs=[
            pl.BlockSpec((sources, slots, width), lambda f: (0, 0, 0)),
            pl.BlockSpec((width, chunk), lambda f: (0, f)),
            pl.BlockSpec((width, chunk), lambda f: (0, f)),
            pl.BlockSpec((chunk, width), lambda f: (f, 0)),
        ],
        out_specs=pl.BlockSpec((sources, parts, slots, share), lambda f: (0, 0, 0, 0)),
        out_shape=jax.ShapeDtypeStruct((sources, parts, slots, share), jnp.bfloat16),
        scratch_shapes=[
            pltpu.VMEM((slots * sources, width), jnp.float32),
        ],
        compiler_params=pltpu.CompilerParams(vmem_limit_bytes=60 * 1024 * 1024),
        cost_estimate=pl.CostEstimate(
            flops=6 * sources * slots * width * ff,
            transcendentals=sources * slots * ff,
            bytes_accessed=2 * (3 * width * ff + 2 * sources * slots * width),
        ),
    )(x, wg, wu, wd)


def local(
    hidden_in,
    queries,
    key_cache,
    cached_value_rows,
    cache_lengths,
    out_weight,
    expert_ids,
    route_probs,
    w_gate,
    w_up,
    w_down,
):
    n_xz = lax.axis_size("x") * lax.axis_size("z")
    n_c = lax.axis_size("c")
    dp_count = n_xz * n_c
    tp_count = lax.axis_size("tensor")
    tp_rank = lax.axis_index("tensor")
    c_rank = lax.axis_index("c")
    rows_dev, kv_local, cache_len, head_dim = key_cache.shape
    groups = queries.shape[1] // (kv_local * head_dim)
    model_width = hidden_in.shape[1]
    col_block = model_width // dp_count
    n_all = dp_count * tp_count

    query_head_count = queries.reshape(rows_dev, kv_local, groups, head_dim)
    scores = jnp.einsum(
        "rhgd,rhld->rhgl", query_head_count, key_cache, preferred_element_type=jnp.float32
    ) * (1.0 / math.sqrt(head_dim))
    valid_mask = (jnp.arange(cache_len, dtype=jnp.int32)[None, :] < cache_lengths[:, None])[
        :, None, None, :
    ]
    scores = jnp.where(valid_mask, scores, -jnp.inf)
    largest = jnp.max(scores, axis=-1, keepdims=True)
    exponent = jnp.exp(scores - largest)
    attn_probs = (exponent / jnp.sum(exponent, axis=-1, keepdims=True)).astype(jnp.bfloat16)
    attn_out = jnp.einsum(
        "rhgl,rhld->rhgd", attn_probs, cached_value_rows, preferred_element_type=jnp.float32
    ).astype(jnp.bfloat16)
    attn_out = attn_out.reshape(rows_dev, kv_local * groups * head_dim)

    w_other = lax.ppermute(out_weight, "c", [(i, (i + 1) % n_c) for i in range(n_c)])
    w_lo = jnp.where(c_rank == 0, out_weight, w_other)
    w_hi = jnp.where(c_rank == 0, w_other, out_weight)
    w_pair = jnp.concatenate([w_lo, w_hi], axis=1)
    sent = jnp.broadcast_to(attn_out[None], (n_xz,) + attn_out.shape)
    mine = lax.all_to_all(sent, ("x", "z"), 0, 0, tiled=True)
    partial_value = jnp.einsum(
        "ird,dc->irc", mine, w_pair, preferred_element_type=jnp.float32
    ).astype(jnp.bfloat16)

    pair_cols = n_c * col_block
    sent = jnp.broadcast_to(partial_value[:, None], (n_xz, tp_count, rows_dev, pair_cols))
    got = lax.all_to_all(
        sent.reshape(n_xz * tp_count, rows_dev, pair_cols), ("x", "z", "tensor"), 0, 0, tiled=True
    )
    projected = got.reshape(n_xz, tp_count, rows_dev, pair_cols).astype(jnp.float32).sum(1)
    projected = projected.transpose(1, 0, 2).reshape(rows_dev, model_width).astype(jnp.bfloat16)
    residual, normed = residual_norm(hidden_in, projected)

    exp_dev = w_gate.shape[0]
    n_exp = n_all * exp_dev
    matches = expert_ids[:, :, None] == jnp.arange(n_exp, dtype=jnp.int32)[None, None, :]
    assigned = jnp.sum(matches.astype(jnp.int32), axis=1)
    slot_rank = jnp.cumsum(assigned, axis=0) - assigned
    slot_hit = (slot_rank[:, :, None] == jnp.arange(CAP, dtype=jnp.int32)[None, None, :]) & (
        assigned[:, :, None] > 0
    )
    route_weights = route_probs / jnp.sum(route_probs, axis=-1, keepdims=True)
    all_weight = jnp.sum(jnp.where(matches, route_weights[:, :, None], 0.0), axis=1)

    hit_col = slot_hit.reshape(rows_dev, dp_count, tp_count, exp_dev, CAP)
    hit_col = lax.dynamic_index_in_dim(hit_col, tp_rank, axis=2, keepdims=False)
    outgoing = jnp.einsum(
        "rmjc,rd->mjcd", hit_col.astype(jnp.bfloat16), normed, preferred_element_type=jnp.float32
    ).astype(jnp.bfloat16)
    arrived_slots = lax.all_to_all(outgoing, DP, 0, 0, tiled=True)
    assert exp_dev == 1
    width_share = model_width // tp_count
    back = expert_ffn(
        arrived_slots.reshape(dp_count, CAP, model_width), w_gate[0], w_up[0], w_down[0], tp_count
    ).reshape(n_all, exp_dev * CAP, width_share)

    results = lax.all_to_all(back, ALL, 0, 0, tiled=True)
    combine_table = jnp.where(slot_hit, all_weight[:, :, None], 0.0)
    mixture = jnp.einsum(
        "rmc,mcd->rd",
        combine_table,
        results.reshape(n_exp, CAP, width_share).astype(jnp.float32),
        precision=lax.Precision.HIGHEST,
    )
    residual_own = lax.dynamic_slice_in_dim(residual, tp_rank * width_share, width_share, 1)
    return (residual_own.astype(jnp.float32) + mixture).astype(jnp.bfloat16)


def split_mesh(mesh):
    devices = np.asarray(mesh.devices)
    n_dp, n_t = devices.shape
    n_c = 2
    try:
        xs = sorted({d.coords[0] for d in devices.flat})
        n_x = len(xs)
    except Exception:
        n_x = 4
    n_z = n_dp // (n_x * n_c)
    return Mesh(devices.reshape(n_x, n_z, n_c, n_t), ALL)


def solution(mesh):
    fine = split_mesh(mesh)
    placed = (
        P(DP, None),
        P(DP, "tensor"),
        P(DP, "tensor", None, None),
        P(DP, "tensor", None, None),
        P(DP),
        P("tensor", DP),
        P(DP, None),
        P(DP, None),
        P(ALL, None, None),
        P(ALL, None, None),
        P(ALL, None, None),
    )
    return jax.shard_map(
        local, mesh=fine, in_specs=placed, out_specs=P(DP, "tensor"), check_vma=False
    )
```
